32 devices in a mesh: layer: 4 (over z), feat: 8 (over y, x, core).
Axes of the slice: x: 2, y: 2, z: 4, core: 2. Of those that a mesh axis runs over, the one named last changes fastest.
Arguments:
- activations: bfloat16 [2, 16, 8, 2304], P(None, 'feat', 'layer'), may hold values from -6 to 6
- enc_weight: bfloat16 [8, 2304, 16384], P('layer', None, 'feat'), may hold values from -0.015625 to 0.015625
- dec_weight: bfloat16 [16384, 8, 2304], P('feat', 'layer'), may hold values from -1 to 1
- enc_bias: float32 [16384], P('feat'), may hold values from -0.5 to 0.5
Outputs:
- enc_step: bfloat16 [8, 2304, 16384], P('layer', None, 'feat')
- dec_step: bfloat16 [16384, 8, 2304], P('feat', 'layer')
- bias_step: float32 [16384], P('feat')
The draws below stay inside these ranges and needn't reach their ends.
All inputs are finite; a program needn't handle non-finite values.
Results may differ from the reference program's by a relative error of at most 0.0095.
Values may be sent and summed in bfloat16 or wider, within the bound.
No kernel may reach another device: no remote copies, remote signals or barrier semaphores. Data moves between devices by JAX's collectives and lax.ppermute only.
A program may use at most 320 MiB of HBM per device.

```python
import jax
import jax.numpy as jnp
from jax import lax

D = 2304
F = 16384
BATCHES = 2
LAYERS = 8
ROWS = 16
N_FEAT = 8


def draw_dec_weight(key, part):
    key_base = jax.random.fold_in(key, 11)
    key_rough = jax.random.fold_in(key, 12)
    layer_pos = jnp.arange(LAYERS, dtype=jnp.float32) / (LAYERS - 1)
    layer_scale = jnp.exp(jnp.log(4.0) * layer_pos)
    rough = jax.random.uniform(key_rough, (F, LAYERS, 1), jnp.float32, 0.7, 1.4)
    base = jnp.clip(jax.random.normal(key_base, (F, LAYERS, D), jnp.float32), -6.0, 6.0)
    values = base * rough * layer_scale[None, :, None] / jnp.sqrt(jnp.float32(F))
    return values.astype(jnp.bfloat16)


def block_scale(key, shape, pieces, smallest, high):
    level = 1.0
    for position, parts in pieces:
        steps = jax.random.uniform(jax.random.fold_in(jax.random.fold_in(key, 6), position), (parts,), jnp.float32, smallest / len(pieces), high / len(pieces))
        level = level * jnp.repeat(jnp.exp(steps), shape[position] // parts).reshape((-1,) + (1,) * (len(shape) - 1 - position))
    return level


def noise(stream_key, extent, spread, limit, cuts=(), kind=jnp.bfloat16):
    factor_of = block_scale(stream_key, extent, cuts, -0.22, 0.18) if cuts else 1.0
    result = jax.random.normal(stream_key, extent, jnp.float32) * spread * factor_of
    return jnp.minimum(jnp.maximum(result, -limit), limit).astype(kind)


def setup_inputs(seed: int = 0) -> dict:
    key_list = jax.random.split(jax.random.key(seed), 5)
    return {
        "activations": noise(key_list[0], (BATCHES, ROWS, LAYERS, D), 1.0, 6.0, ((1, 8), (2, 4))),
        "enc_weight": noise(key_list[1], (LAYERS, D, F), (0.3333 * (LAYERS * D) ** -0.5), 0.015625, ((0, 4), (2, 8))),
        "dec_weight": draw_dec_weight(jax.random.fold_in(key_list[4], 71), 0),
        "enc_bias": jnp.clip(jax.random.uniform(key_list[3], (F,), jnp.float32, -0.5, 0.5) * block_scale(key_list[3], (F,), ((0, 8),), -0.4, 0.0), -0.5, 0.5),
    }


rate = 0.01
penalty = 2.0
eps = 1e-06

def normalize(x):
    xf = x.astype(jnp.float32)
    scale = jnp.sqrt(lax.optimization_barrier(jnp.mean(xf * xf, axis=-1, keepdims=True)) + eps)
    return (xf / scale).astype(jnp.bfloat16)

def block_forward(we, be, xk):
    pre = jnp.dot(xk, we.astype(jnp.bfloat16), preferred_element_type=jnp.float32) + be
    pos = jnp.maximum(pre, 0.0)
    return (pos, pos * pos)

def block_grads(we, wd, be, xk, errb, lay, width):
    batch = xk.shape[0]
    fblk = wd.shape[0]
    pos, act = block_forward(we, be, xk)
    wd3 = wd.reshape(fblk, lay, width)
    lens = jnp.sqrt(lax.optimization_barrier(jnp.sum(wd3 * wd3, axis=-1)) + eps)
    total = lax.optimization_barrier(jnp.sum(lens, axis=-1))
    dims = (((1,), (1,)), ((), ()))
    dact = 2.0 / batch * lax.dot_general(errb, wd.astype(jnp.bfloat16), dims, preferred_element_type=jnp.float32) + penalty / batch * total
    dpre = dact * 2.0 * pos
    rowdims = (((0,), (0,)), ((), ()))
    gwe = lax.dot_general(xk, dpre.astype(jnp.bfloat16), rowdims, preferred_element_type=jnp.float32)
    actsum = lax.optimization_barrier(jnp.sum(act, axis=0))
    gwd = 2.0 / batch * lax.dot_general(act.astype(jnp.bfloat16), errb, rowdims, preferred_element_type=jnp.float32)
    gwd = gwd + (penalty / batch * actsum[:, None, None] * wd3 / lens[:, :, None]).reshape(fblk, lay * width)
    gbe = lax.optimization_barrier(jnp.sum(dpre, axis=0))
    return (gwe, gwd, gbe)

def reference(activations, enc_weight, dec_weight, enc_bias):
    nb, rows, lay, width = activations.shape
    feats = enc_weight.shape[2]
    lw = lay * width
    blocks = N_FEAT
    fblk = feats // blocks
    normed = normalize(activations).reshape(nb, rows, lw)
    we_blocks = enc_weight.reshape(lw, blocks, fblk).transpose(1, 0, 2)
    wd_blocks = dec_weight.reshape(blocks, fblk, lw)
    be_blocks = enc_bias.reshape(blocks, fblk)

    def first_weights(blk):
        return (we_blocks[blk].astype(jnp.float32), wd_blocks[blk].astype(jnp.float32), be_blocks[blk].astype(jnp.float32))

    def errors(getw, xk):

        def step(acc, blk):
            we, wd, be = getw(blk)
            pos, act = block_forward(we, be, xk)
            return (acc + jnp.dot(act.astype(jnp.bfloat16), wd.astype(jnp.bfloat16), preferred_element_type=jnp.float32), None)
        recon, _ = lax.scan(step, jnp.zeros((rows, lw), jnp.float32), jnp.arange(blocks))
        return (recon - normed_f(xk)).astype(jnp.bfloat16)

    def normed_f(xk):
        return xk.astype(jnp.float32)
    errb0 = errors(first_weights, normed[0])

    def second_weights(blk):
        we, wd, be = first_weights(blk)
        gwe, gwd, gbe = block_grads(we, wd, be, normed[0], errb0, lay, width)
        return (we - rate * gwe, wd - rate * gwd, be - rate * gbe)
    errb1 = errors(second_weights, normed[1])

    def final(blk):
        we, wd, be = first_weights(blk)
        g0 = block_grads(we, wd, be, normed[0], errb0, lay, width)
        we1, wd1, be1 = (we - rate * g0[0], wd - rate * g0[1], be - rate * g0[2])
        g1 = block_grads(we1, wd1, be1, normed[1], errb1, lay, width)
        return ((g0[0] + g1[0]).astype(jnp.bfloat16), (g0[1] + g1[1]).astype(jnp.bfloat16), g0[2] + g1[2])
    enc_blocks, dec_blocks, bias_blocks = lax.map(final, jnp.arange(blocks))
    enc_step = enc_blocks.transpose(1, 0, 2).reshape(lay, width, feats)
    dec_step = dec_blocks.reshape(feats, lay, width)
    bias_step = bias_blocks.reshape(feats)
    return (enc_step, dec_step, bias_step)
```

```python
import jax
import jax.numpy as jnp
from jax import lax
from jax.sharding import PartitionSpec as P

rate = 0.01
penalty = 2.0
eps = 1e-06
HI = lax.Precision.HIGHEST


def normalize(x):
    xf = x.astype(jnp.float32)
    scale = jnp.sqrt(jnp.mean(xf * xf, axis=-1, keepdims=True) + eps)
    return (xf / scale).astype(jnp.bfloat16)


def allreduce(x, axis, n):
    k = 1
    while k < n:
        x = x + lax.ppermute(x, axis, [(i, i ^ k) for i in range(n)])
        k *= 2
    return x


def allgather_rows(x, axis, n):
    me = lax.axis_index(axis)
    k = 1
    while k < n:
        got = lax.ppermute(x, axis, [(i, i ^ k) for i in range(n)])
        low = (me // k) % 2 == 0
        x = jnp.where(low, jnp.concatenate([x, got], axis=1), jnp.concatenate([got, x], axis=1))
        k *= 2
    return x


def split_bf16(v):
    hi = v.astype(jnp.bfloat16)
    lo = (v - hi.astype(jnp.float32)).astype(jnp.bfloat16)
    return hi, lo


def block_rows(e, lay, width):
    rows = e.shape[0]
    e3 = e.reshape(rows, lay, width)
    eye = jnp.eye(lay, dtype=e.dtype)
    blk = eye[:, None, :, None] * e3[None, :, :, :]
    return blk.reshape(lay * rows, lay * width)


def per_layer_dot(e, wd_flat, lay, width):
    rows = e.shape[0]
    blk = block_rows(e, lay, width)
    out = lax.dot_general(blk, wd_flat, (((1,), (1,)), ((), ())), preferred_element_type=jnp.float32)
    return out.reshape(lay, rows, wd_flat.shape[0])


def per_layer_lhs_dot(a, wd_flat, lay, width):
    rows = a.shape[1]
    hi, lo = split_bf16(a)
    lhs = jnp.concatenate([hi, lo], axis=1).reshape(lay * 2 * rows, -1)
    out = jnp.dot(lhs, wd_flat, preferred_element_type=jnp.float32)
    out = out.reshape(lay, 2, rows, lay, width)
    idx = jnp.arange(lay)
    diag = out[idx, :, :, idx, :]
    diag = diag[:, 0] + diag[:, 1]
    return diag.transpose(1, 0, 2).reshape(rows, lay * width)


def per_device(activations, enc_weight, dec_weight, enc_bias, n_layer, n_feat):
    nb, rloc, lay, width = activations.shape
    feats = enc_weight.shape[2]
    lw = lay * width
    rows = rloc * n_feat
    cst = 2.0 / rows
    pen = penalty / rows
    c1 = rate * cst

    xn = normalize(activations).reshape(nb, rloc, lw)
    xg = allgather_rows(xn, "feat", n_feat)
    x0, x1 = xg[0], xg[1]
    x0f = x0.astype(jnp.float32)
    x1f = x1.astype(jnp.float32)

    we_flat = enc_weight.reshape(lw, feats)
    wd_flat = dec_weight.reshape(feats, lw)
    wd3f = dec_weight.astype(jnp.float32)

    pre_part = jnp.dot(xg.reshape(nb * rows, lw), we_flat, preferred_element_type=jnp.float32)
    gram = lax.dot_general(x1, x0, (((1,), (1,)), ((), ())), preferred_element_type=jnp.float32)
    gk = -(-(rows * rows) // feats)
    gpad = jnp.pad(gram.reshape(-1), (0, gk * feats - rows * rows)).reshape(gk, feats)
    red1 = allreduce(jnp.concatenate([pre_part, gpad], axis=0), "layer", n_layer)
    pre_x0 = red1[:rows]
    pre_x1 = red1[rows : 2 * rows]
    gram10 = red1[2 * rows :].reshape(-1)[: rows * rows].reshape(rows, rows)

    sq0 = jnp.sum(wd3f * wd3f, axis=-1)
    lens0 = jnp.sqrt(sq0 + eps)

    pre0 = pre_x0 + enc_bias
    pos0 = jnp.maximum(pre0, 0.0)
    act0 = pos0 * pos0
    actb0 = act0.astype(jnp.bfloat16)
    asum0 = jnp.sum(act0, axis=0)
    rec0 = allreduce(jnp.dot(actb0, wd_flat, preferred_element_type=jnp.float32), "feat", n_feat)
    errb0 = (rec0 - x0f).astype(jnp.bfloat16)
    d0 = per_layer_dot(errb0, wd_flat, lay, width)
    dact0_part = cst * jnp.sum(d0, axis=0) + pen * jnp.sum(lens0, axis=1)[None, :]
    dact0 = allreduce(dact0_part, "layer", n_layer)
    dpre0 = dact0 * 2.0 * pos0
    dpreb0 = dpre0.astype(jnp.bfloat16)
    gbe0 = jnp.sum(dpre0, axis=0)

    s0 = 1.0 - rate * pen * asum0[:, None] / lens0
    be1 = enc_bias - rate * gbe0
    corr = jnp.dot(gram10, dpreb0.astype(jnp.float32), precision=HI)
    pre1 = pre_x1 - rate * corr + be1
    pos1 = jnp.maximum(pre1, 0.0)
    act1 = pos1 * pos1
    actb1 = act1.astype(jnp.bfloat16)
    asum1 = jnp.sum(act1, axis=0)
    actb0f = actb0.astype(jnp.float32)
    actb1f = actb1.astype(jnp.float32)
    a1 = actb1f[None, :, :] * s0.T[:, None, :]
    h10 = jnp.dot(actb1f, actb0f.T, precision=HI)
    rec1_part = per_layer_lhs_dot(a1, wd_flat, lay, width) - c1 * jnp.dot(h10, errb0.astype(jnp.float32), precision=HI)
    rec1 = allreduce(rec1_part, "feat", n_feat)
    errb1 = (rec1 - x1f).astype(jnp.bfloat16)

    e0f = errb0.astype(jnp.float32).reshape(rows, lay, width)
    e1f = errb1.astype(jnp.float32).reshape(rows, lay, width)
    g00 = jnp.einsum("rld,sld->lrs", e0f, e0f, precision=HI)
    g10 = jnp.einsum("rld,sld->lrs", e1f, e0f, precision=HI)
    cross = jnp.einsum("rj,lrj->jl", actb0f, d0, precision=HI)
    quad = jnp.einsum("rj,lrs,sj->jl", actb0f, g00, actb0f, precision=HI)
    sq1 = s0 * s0 * sq0 - 2.0 * c1 * s0 * cross + c1 * c1 * quad
    lens1 = jnp.sqrt(jnp.maximum(sq1, 0.0) + eps)

    d1 = per_layer_dot(errb1, wd_flat, lay, width)
    lowr = jnp.einsum("lrs,sj->lrj", g10, actb0f, precision=HI)
    dd1 = s0.T[:, None, :] * d1 - c1 * lowr
    dact1_part = cst * jnp.sum(dd1, axis=0) + pen * jnp.sum(lens1, axis=1)[None, :]

    g0 = cst - pen * c1 * asum1[:, None] / lens1
    hcoef = pen * (asum0[:, None] / lens0 + asum1[:, None] * s0 / lens1)
    lhs0 = g0.T[:, :, None] * actb0f.T[None, :, :]
    hi0, lo0 = split_bf16(lhs0)
    lhs1 = jnp.broadcast_to((cst * actb1f).T.astype(jnp.bfloat16)[None], (lay, feats, rows))
    lhs = jnp.concatenate([lhs1, hi0, lo0], axis=2)
    rhs = jnp.concatenate([errb1, errb0, errb0], axis=0)
    rhs_blk = block_rows(rhs, lay, width)
    lhs_cat = lhs.transpose(1, 0, 2).reshape(feats, lay * 3 * rows)
    dec = jnp.dot(lhs_cat, rhs_blk, preferred_element_type=jnp.float32)
    hfull = jnp.repeat(hcoef, width, axis=1)
    dec_step = (dec + hfull * wd_flat.astype(jnp.float32)).astype(jnp.bfloat16).reshape(feats, lay, width)

    dact1 = allreduce(dact1_part, "layer", n_layer)
    dpre1 = dact1 * 2.0 * pos1
    dpreb1 = dpre1.astype(jnp.bfloat16)
    gbe1 = jnp.sum(dpre1, axis=0)

    dp = jnp.concatenate([dpreb0, dpreb1], axis=0)
    enc = lax.dot_general(xg.reshape(nb * rows, lw), dp, (((0,), (0,)), ((), ())), preferred_element_type=jnp.float32)
    enc_step = enc.astype(jnp.bfloat16).reshape(lay, width, feats)
    bias_step = gbe0 + gbe1
    return (enc_step, dec_step, bias_step)


def solution(mesh):
    n_layer = mesh.shape["layer"]
    n_feat = mesh.shape["feat"]
    in_specs = (
        P(None, "feat", "layer", None),
        P("layer", None, "feat"),
        P("feat", "layer", None),
        P("feat"),
    )
    out_specs = (P("layer", None, "feat"), P("feat", "layer", None), P("feat"))

    def body(a, we, wd, be):
        return per_device(a, we, wd, be, n_layer, n_feat)

    return jax.shard_map(body, mesh=mesh, in_specs=in_specs, out_specs=out_specs, check_vma=False)
```

```python
import jax
import jax.numpy as jnp
from jax import lax
from jax.sharding import PartitionSpec as P

rate = 0.01
penalty = 2.0
eps = 1e-06
HI = lax.Precision.HIGHEST


def normalize(x):
    xf = x.astype(jnp.float32)
    scale = jnp.sqrt(jnp.mean(xf * xf, axis=-1, keepdims=True) + eps)
    return (xf / scale).astype(jnp.bfloat16)


def allreduce(x, axis, n):
    k = 1
    while k < n:
        x = x + lax.ppermute(x, axis, [(i, i ^ k) for i in range(n)])
        k *= 2
    return x


def allgather_rows(x, axis, n):
    me = lax.axis_index(axis)
    k = 1
    while k < n:
        got = lax.ppermute(x, axis, [(i, i ^ k) for i in range(n)])
        low = (me // k) % 2 == 0
        x = jnp.where(low, jnp.concatenate([x, got], axis=1), jnp.concatenate([got, x], axis=1))
        k *= 2
    return x


def split_bf16(v):
    hi = v.astype(jnp.bfloat16)
    lo = (v - hi.astype(jnp.float32)).astype(jnp.bfloat16)
    return hi, lo


def block_rows(e, lay, width):
    rows = e.shape[0]
    e3 = e.reshape(rows, lay, width)
    eye = jnp.eye(lay, dtype=e.dtype)
    blk = eye[:, None, :, None] * e3[None, :, :, :]
    return blk.reshape(lay * rows, lay * width)


def per_layer_dot(e, wd2, lay, width):
    rows = e.shape[0]
    blk = block_rows(e, lay, width)
    out = lax.dot_general(wd2, blk, (((1,), (1,)), ((), ())), preferred_element_type=jnp.float32)
    return out.reshape(wd2.shape[0], lay, rows).transpose(1, 2, 0)


def per_layer_lhs_dot(a, wd2, lay, width):
    rows = a.shape[1]
    hi, lo = split_bf16(a)
    lhs = jnp.concatenate([hi, lo], axis=1).reshape(lay * 2 * rows, -1)
    out = jnp.dot(lhs, wd2, preferred_element_type=jnp.float32)
    parts = []
    for l in range(lay):
        blk = out[l * 2 * rows : (l + 1) * 2 * rows, l * width : (l + 1) * width]
        parts.append(blk[:rows] + blk[rows:])
    return jnp.concatenate(parts, axis=1)


def per_device(activations, enc_weight, dec_weight, enc_bias, n_layer, n_feat):
    nb, rloc, lay, width = activations.shape
    feats = enc_weight.shape[2]
    lw = lay * width
    rows = rloc * n_feat
    cst = 2.0 / rows
    pen = penalty / rows
    c1 = rate * cst

    xn = normalize(activations).reshape(nb, rloc, lw)
    xg = allgather_rows(xn, "feat", n_feat)
    x0, x1 = xg[0], xg[1]
    x0f = x0.astype(jnp.float32)
    x1f = x1.astype(jnp.float32)

    we_flat = enc_weight.reshape(lw, feats)
    wd_flat = dec_weight.reshape(feats, lw)

    pre_part = jnp.dot(xg.reshape(nb * rows, lw), we_flat, preferred_element_type=jnp.float32)
    gram = lax.dot_general(x1, x0, (((1,), (1,)), ((), ())), preferred_element_type=jnp.float32)
    gk = -(-(rows * rows) // feats)
    gpad = jnp.pad(gram.reshape(-1), (0, gk * feats - rows * rows)).reshape(gk, feats)
    red1 = allreduce(jnp.concatenate([pre_part, gpad], axis=0), "layer", n_layer)
    pre_x0 = red1[:rows]
    pre_x1 = red1[rows : 2 * rows]
    gram10 = red1[2 * rows :].reshape(-1)[: rows * rows].reshape(rows, rows)

    sq0 = jnp.stack(
        [jnp.sum(jnp.square(wd_flat[:, l * width : (l + 1) * width].astype(jnp.float32)), axis=1) for l in range(lay)],
        axis=1,
    )
    lens0 = jnp.sqrt(sq0 + eps)

    pre0 = pre_x0 + enc_bias
    pos0 = jnp.maximum(pre0, 0.0)
    act0 = pos0 * pos0
    actb0 = act0.astype(jnp.bfloat16)
    asum0 = jnp.sum(act0, axis=0)
    rec0 = allreduce(jnp.dot(actb0, wd_flat, preferred_element_type=jnp.float32), "feat", n_feat)
    errb0 = (rec0 - x0f).astype(jnp.bfloat16)
    d0 = per_layer_dot(errb0, wd_flat, lay, width)
    dact0_part = cst * jnp.sum(d0, axis=0) + pen * jnp.sum(lens0, axis=1)[None, :]
    dact0 = allreduce(dact0_part, "layer", n_layer)
    dpre0 = dact0 * 2.0 * pos0
    dpreb0 = dpre0.astype(jnp.bfloat16)
    gbe0 = jnp.sum(dpre0, axis=0)

    s0 = 1.0 - rate * pen * asum0[:, None] / lens0
    be1 = enc_bias - rate * gbe0
    corr = jnp.dot(gram10, dpreb0.astype(jnp.float32), precision=HI)
    pre1 = pre_x1 - rate * corr + be1
    pos1 = jnp.maximum(pre1, 0.0)
    act1 = pos1 * pos1
    actb1 = act1.astype(jnp.bfloat16)
    asum1 = jnp.sum(act1, axis=0)
    actb0f = actb0.astype(jnp.float32)
    actb1f = actb1.astype(jnp.float32)
    a1 = actb1f[None, :, :] * s0.T[:, None, :]
    h10 = jnp.dot(actb1f, actb0f.T, precision=HI)
    rec1_part = per_layer_lhs_dot(a1, wd_flat, lay, width) - c1 * jnp.dot(h10, errb0.astype(jnp.float32), precision=HI)
    rec1 = allreduce(rec1_part, "feat", n_feat)
    errb1 = (rec1 - x1f).astype(jnp.bfloat16)

    e0f = errb0.astype(jnp.float32).reshape(rows, lay, width)
    e1f = errb1.astype(jnp.float32).reshape(rows, lay, width)
    g00 = jnp.einsum("rld,sld->lrs", e0f, e0f, precision=HI)
    g10 = jnp.einsum("rld,sld->lrs", e1f, e0f, precision=HI)
    cross = jnp.einsum("rj,lrj->jl", actb0f, d0, precision=HI)
    quad = jnp.einsum("rj,lrs,sj->jl", actb0f, g00, actb0f, precision=HI)
    sq1 = s0 * s0 * sq0 - 2.0 * c1 * s0 * cross + c1 * c1 * quad
    lens1 = jnp.sqrt(jnp.maximum(sq1, 0.0) + eps)

    d1 = per_layer_dot(errb1, wd_flat, lay, width)
    lowr = jnp.einsum("lrs,sj->lrj", g10, actb0f, precision=HI)
    dd1 = s0.T[:, None, :] * d1 - c1 * lowr
    dact1_part = cst * jnp.sum(dd1, axis=0) + pen * jnp.sum(lens1, axis=1)[None, :]

    g0 = cst - pen * c1 * asum1[:, None] / lens1
    hcoef = pen * (asum0[:, None] / lens0 + asum1[:, None] * s0 / lens1)
    lhs0 = g0.T[:, :, None] * actb0f.T[None, :, :]
    hi0, lo0 = split_bf16(lhs0)
    lhs1 = jnp.broadcast_to((cst * actb1f).T.astype(jnp.bfloat16)[None], (lay, feats, rows))
    lhs = jnp.concatenate([lhs1, hi0, lo0], axis=2)
    rhs = jnp.concatenate([errb1, errb0, errb0], axis=0)
    rhs_blk = block_rows(rhs, lay, width)
    lhs_cat = lhs.transpose(1, 0, 2).reshape(feats, lay * 3 * rows)
    rhs3 = rhs_blk.reshape(lay * 3 * rows, lay, width)
    dec = lax.dot_general(lhs_cat, rhs3, (((1,), (0,)), ((), ())), preferred_element_type=jnp.float32)
    dec = dec + hcoef[:, :, None] * dec_weight.astype(jnp.float32)
    dec_step = dec.astype(jnp.bfloat16)

    dact1 = allreduce(dact1_part, "layer", n_layer)
    dpre1 = dact1 * 2.0 * pos1
    dpreb1 = dpre1.astype(jnp.bfloat16)
    gbe1 = jnp.sum(dpre1, axis=0)

    dp = jnp.concatenate([dpreb0, dpreb1], axis=0)
    enc = lax.dot_general(xg.reshape(nb * rows, lw), dp, (((0,), (0,)), ((), ())), preferred_element_type=jnp.float32)
    enc_step = enc.astype(jnp.bfloat16).reshape(lay, width, feats)
    bias_step = gbe0 + gbe1
    return (enc_step, dec_step, bias_step)


def solution(mesh):
    n_layer = mesh.shape["layer"]
    n_feat = mesh.shape["feat"]
    in_specs = (
        P(None, "feat", "layer", None),
        P("layer", None, "feat"),
        P("feat", "layer", None),
        P("feat"),
    )
    out_specs = (P("layer", None, "feat"), P("feat", "layer", None), P("feat"))

    def body(a, we, wd, be):
        return per_device(a, we, wd, be, n_layer, n_feat)

    return jax.shard_map(body, mesh=mesh, in_specs=in_specs, out_specs=out_specs, check_vma=False)
```

```python
import jax
import jax.numpy as jnp
from jax import lax
from jax.experimental import pallas as pl
from jax.sharding import PartitionSpec as P

rate = 0.01
penalty = 2.0
eps = 1e-06
HI = lax.Precision.HIGHEST


def normalize(x):
    xf = x.astype(jnp.float32)
    scale = jnp.sqrt(jnp.mean(xf * xf, axis=-1, keepdims=True) + eps)
    return (xf / scale).astype(jnp.bfloat16)


def allreduce(x, axis, n):
    k = 1
    while k < n:
        x = x + lax.ppermute(x, axis, [(i, i ^ k) for i in range(n)])
        k *= 2
    return x


def allgather_rows(x, axis, n):
    me = lax.axis_index(axis)
    k = 1
    while k < n:
        got = lax.ppermute(x, axis, [(i, i ^ k) for i in range(n)])
        low = (me // k) % 2 == 0
        x = jnp.where(low, jnp.concatenate([x, got], axis=1), jnp.concatenate([got, x], axis=1))
        k *= 2
    return x


def split_bf16(v):
    hi = v.astype(jnp.bfloat16)
    lo = (v - hi.astype(jnp.float32)).astype(jnp.bfloat16)
    return hi, lo


def block_rows(e, lay, width):
    rows = e.shape[0]
    e3 = e.reshape(rows, lay, width)
    eye = jnp.eye(lay, dtype=e.dtype)
    blk = eye[:, None, :, None] * e3[None, :, :, :]
    return blk.reshape(lay * rows, lay * width)


def per_layer_dot(e, wd2, lay, width):
    rows = e.shape[0]
    blk = block_rows(e, lay, width)
    out = lax.dot_general(wd2, blk, (((1,), (1,)), ((), ())), preferred_element_type=jnp.float32)
    return out.reshape(wd2.shape[0], lay, rows).transpose(1, 2, 0)


def per_layer_lhs_dot(a, wd2, lay, width):
    rows = a.shape[1]
    hi, lo = split_bf16(a)
    lhs = jnp.concatenate([hi, lo], axis=1).reshape(lay * 2 * rows, -1)
    out = jnp.dot(lhs, wd2, preferred_element_type=jnp.float32)
    parts = []
    for l in range(lay):
        blk = out[l * 2 * rows : (l + 1) * 2 * rows, l * width : (l + 1) * width]
        parts.append(blk[:rows] + blk[rows:])
    return jnp.concatenate(parts, axis=1)


def dec_kernel(lhs_ref, rhs_ref, h_ref, wd_ref, out_ref):
    for l in range(wd_ref.shape[1]):
        acc = jnp.dot(lhs_ref[l], rhs_ref[l], preferred_element_type=jnp.float32)
        acc = acc + h_ref[:, l : l + 1] * wd_ref[:, l, :].astype(jnp.float32)
        out_ref[:, l, :] = acc.astype(out_ref.dtype)


def dec_call(lhs, rhs, hcoef, wd):
    lay, feats, k = lhs.shape
    width = rhs.shape[2]
    tj = min(256, feats)
    cost = pl.CostEstimate(
        flops=2 * feats * lay * width * k, transcendentals=0, bytes_accessed=4 * feats * lay * width
    )
    return pl.pallas_call(
        dec_kernel,
        grid=(feats // tj,),
        in_specs=[
            pl.BlockSpec((lay, tj, k), lambda j: (0, j, 0)),
            pl.BlockSpec((lay, k, width), lambda j: (0, 0, 0)),
            pl.BlockSpec((tj, lay), lambda j: (j, 0)),
            pl.BlockSpec((tj, lay, width), lambda j: (j, 0, 0)),
        ],
        out_specs=pl.BlockSpec((tj, lay, width), lambda j: (j, 0, 0)),
        out_shape=jax.ShapeDtypeStruct((feats, lay, width), jnp.bfloat16),
        cost_estimate=cost,
    )(lhs, rhs, hcoef, wd)


def per_device(activations, enc_weight, dec_weight, enc_bias, n_layer, n_feat):
    nb, rloc, lay, width = activations.shape
    feats = enc_weight.shape[2]
    lw = lay * width
    rows = rloc * n_feat
    cst = 2.0 / rows
    pen = penalty / rows
    c1 = rate * cst

    xn = normalize(activations).reshape(nb, rloc, lw)
    xg = allgather_rows(xn, "feat", n_feat)
    x0, x1 = xg[0], xg[1]
    x0f = x0.astype(jnp.float32)
    x1f = x1.astype(jnp.float32)

    we_flat = enc_weight.reshape(lw, feats)
    wd_flat = dec_weight.reshape(feats, lw)

    pre_part = jnp.dot(xg.reshape(nb * rows, lw), we_flat, preferred_element_type=jnp.float32)
    gram = lax.dot_general(x1, x0, (((1,), (1,)), ((), ())), preferred_element_type=jnp.float32)
    gk = -(-(rows * rows) // feats)
    gpad = jnp.pad(gram.reshape(-1), (0, gk * feats - rows * rows)).reshape(gk, feats)
    red1 = allreduce(jnp.concatenate([pre_part, gpad], axis=0), "layer", n_layer)
    pre_x0 = red1[:rows]
    pre_x1 = red1[rows : 2 * rows]
    gram10 = red1[2 * rows :].reshape(-1)[: rows * rows].reshape(rows, rows)

    sq0 = jnp.stack(
        [jnp.sum(jnp.square(wd_flat[:, l * width : (l + 1) * width].astype(jnp.float32)), axis=1) for l in range(lay)],
        axis=1,
    )
    lens0 = jnp.sqrt(sq0 + eps)

    pre0 = pre_x0 + enc_bias
    pos0 = jnp.maximum(pre0, 0.0)
    act0 = pos0 * pos0
    actb0 = act0.astype(jnp.bfloat16)
    asum0 = jnp.sum(act0, axis=0)
    rec0 = allreduce(jnp.dot(actb0, wd_flat, preferred_element_type=jnp.float32), "feat", n_feat)
    errb0 = (rec0 - x0f).astype(jnp.bfloat16)
    d0 = per_layer_dot(errb0, wd_flat, lay, width)
    dact0_part = cst * jnp.sum(d0, axis=0) + pen * jnp.sum(lens0, axis=1)[None, :]
    dact0 = allreduce(dact0_part, "layer", n_layer)
    dpre0 = dact0 * 2.0 * pos0
    dpreb0 = dpre0.astype(jnp.bfloat16)
    gbe0 = jnp.sum(dpre0, axis=0)

    s0 = 1.0 - rate * pen * asum0[:, None] / lens0
    be1 = enc_bias - rate * gbe0
    corr = jnp.dot(gram10, dpreb0.astype(jnp.float32), precision=HI)
    pre1 = pre_x1 - rate * corr + be1
    pos1 = jnp.maximum(pre1, 0.0)
    act1 = pos1 * pos1
    actb1 = act1.astype(jnp.bfloat16)
    asum1 = jnp.sum(act1, axis=0)
    actb0f = actb0.astype(jnp.float32)
    actb1f = actb1.astype(jnp.float32)
    a1 = actb1f[None, :, :] * s0.T[:, None, :]
    h10 = jnp.dot(actb1f, actb0f.T, precision=HI)
    rec1_part = per_layer_lhs_dot(a1, wd_flat, lay, width) - c1 * jnp.dot(h10, errb0.astype(jnp.float32), precision=HI)
    rec1 = allreduce(rec1_part, "feat", n_feat)
    errb1 = (rec1 - x1f).astype(jnp.bfloat16)

    e0f = errb0.astype(jnp.float32).reshape(rows, lay, width)
    e1f = errb1.astype(jnp.float32).reshape(rows, lay, width)
    g00 = jnp.einsum("rld,sld->lrs", e0f, e0f, precision=HI)
    g10 = jnp.einsum("rld,sld->lrs", e1f, e0f, precision=HI)
    cross = jnp.einsum("rj,lrj->jl", actb0f, d0, precision=HI)
    quad = jnp.einsum("rj,lrs,sj->jl", actb0f, g00, actb0f, precision=HI)
    sq1 = s0 * s0 * sq0 - 2.0 * c1 * s0 * cross + c1 * c1 * quad
    lens1 = jnp.sqrt(jnp.maximum(sq1, 0.0) + eps)

    d1 = per_layer_dot(errb1, wd_flat, lay, width)
    lowr = jnp.einsum("lrs,sj->lrj", g10, actb0f, precision=HI)
    dd1 = s0.T[:, None, :] * d1 - c1 * lowr
    dact1_part = cst * jnp.sum(dd1, axis=0) + pen * jnp.sum(lens1, axis=1)[None, :]

    g0 = cst - pen * c1 * asum1[:, None] / lens1
    hcoef = pen * (asum0[:, None] / lens0 + asum1[:, None] * s0 / lens1)
    lhs0 = g0.T[:, :, None] * actb0f.T[None, :, :]
    hi0, lo0 = split_bf16(lhs0)
    lhs1 = jnp.broadcast_to((cst * actb1f).T.astype(jnp.bfloat16)[None], (lay, feats, rows))
    lhs = jnp.concatenate([lhs1, hi0, lo0], axis=2)
    rhs = jnp.concatenate([errb1, errb0, errb0], axis=0)
    rhs3 = rhs.reshape(3 * rows, lay, width).transpose(1, 0, 2)
    dact1_part, lhs, rhs3, hcoef = lax.optimization_barrier((dact1_part, lhs, rhs3, hcoef))
    dec_step = dec_call(lhs, rhs3, hcoef, dec_weight)
    dact1 = allreduce(dact1_part, "layer", n_layer)
    dact1, dec_step = lax.optimization_barrier((dact1, dec_step))
    dpre1 = dact1 * 2.0 * pos1
    dpreb1 = dpre1.astype(jnp.bfloat16)
    gbe1 = jnp.sum(dpre1, axis=0)

    dp = jnp.concatenate([dpreb0, dpreb1], axis=0)
    enc = lax.dot_general(xg.reshape(nb * rows, lw), dp, (((0,), (0,)), ((), ())), preferred_element_type=jnp.float32)
    enc_step = enc.astype(jnp.bfloat16).reshape(lay, width, feats)
    bias_step = gbe0 + gbe1
    return (enc_step, dec_step, bias_step)


def solution(mesh):
    n_layer = mesh.shape["layer"]
    n_feat = mesh.shape["feat"]
    in_specs = (
        P(None, "feat", "layer", None),
        P("layer", None, "feat"),
        P("feat", "layer", None),
        P("feat"),
    )
    out_specs = (P("layer", None, "feat"), P("feat", "layer", None), P("feat"))

    def body(a, we, wd, be):
        return per_device(a, we, wd, be, n_layer, n_feat)

    return jax.shard_map(body, mesh=mesh, in_specs=in_specs, out_specs=out_specs, check_vma=False)
```

```python
import jax
import jax.numpy as jnp
from jax import lax
from jax.experimental import pallas as pl
from jax.sharding import PartitionSpec as P

rate = 0.01
penalty = 2.0
eps = 1e-06
HI = lax.Precision.HIGHEST


def normalize(x):
    xf = x.astype(jnp.float32)
    scale = jnp.sqrt(jnp.mean(xf * xf, axis=-1, keepdims=True) + eps)
    return (xf / scale).astype(jnp.bfloat16)


def allreduce(x, axis, n):
    k = 1
    while k < n:
        x = x + lax.ppermute(x, axis, [(i, i ^ k) for i in range(n)])
        k *= 2
    return x


def allgather_rows(x, axis, n):
    me = lax.axis_index(axis)
    k = 1
    while k < n:
        got = lax.ppermute(x, axis, [(i, i ^ k) for i in range(n)])
        low = (me // k) % 2 == 0
        x = jnp.where(low, jnp.concatenate([x, got], axis=1), jnp.concatenate([got, x], axis=1))
        k *= 2
    return x


def split_bf16(v):
    hi = v.astype(jnp.bfloat16)
    lo = (v - hi.astype(jnp.float32)).astype(jnp.bfloat16)
    return hi, lo


def block_rows(e, lay, width):
    rows = e.shape[0]
    e3 = e.reshape(rows, lay, width)
    eye = jnp.eye(lay, dtype=e.dtype)
    blk = eye[:, None, :, None] * e3[None, :, :, :]
    return blk.reshape(lay * rows, lay * width)


def per_layer_dot(e, wd2, lay, width):
    rows = e.shape[0]
    blk = block_rows(e, lay, width)
    out = lax.dot_general(wd2, blk, (((1,), (1,)), ((), ())), preferred_element_type=jnp.float32)
    return out.reshape(wd2.shape[0], lay, rows).transpose(1, 2, 0)


def rec1_dot(actb1, delta, wd2, lay, width):
    rows = actb1.shape[0]
    corr = [(actb1.astype(jnp.float32) * delta[:, l][None, :]).astype(jnp.bfloat16) for l in range(lay)]
    lhs = jnp.concatenate([actb1] + corr, axis=0)
    out = jnp.dot(lhs, wd2, preferred_element_type=jnp.float32)
    parts = []
    for l in range(lay):
        cols = slice(l * width, (l + 1) * width)
        parts.append(out[:rows, cols] + out[(l + 1) * rows : (l + 2) * rows, cols])
    return jnp.concatenate(parts, axis=1)


def dec_kernel(lhs_ref, rhs_ref, h_ref, wd_ref, out_ref):
    tj, lay, width = wd_ref.shape
    acc = jnp.dot(lhs_ref[...], rhs_ref[...], preferred_element_type=jnp.float32)
    w = wd_ref[...].reshape(tj * lay, width).astype(jnp.float32)
    acc = acc + h_ref[...] * w
    out_ref[...] = acc.astype(out_ref.dtype).reshape(tj, lay, width)


def dec_call(lhs, rhs, hcoef, wd):
    lay, feats, k = lhs.shape
    width = rhs.shape[2]
    tj = min(256, feats)
    eye = jnp.eye(lay, dtype=lhs.dtype)
    lhs_int = (eye[None, :, :, None] * lhs.transpose(1, 0, 2)[:, :, None, :]).reshape(feats * lay, lay * k)
    rhs_st = rhs.reshape(lay * k, width)
    h_int = hcoef.reshape(feats * lay, 1)
    cost = pl.CostEstimate(
        flops=2 * feats * lay * width * k * lay, transcendentals=0, bytes_accessed=4 * feats * lay * width
    )
    return pl.pallas_call(
        dec_kernel,
        grid=(feats // tj,),
        in_specs=[
            pl.BlockSpec((tj * lay, lay * k), lambda j: (j, 0)),
            pl.BlockSpec((lay * k, width), lambda j: (0, 0)),
            pl.BlockSpec((tj * lay, 1), lambda j: (j, 0)),
            pl.BlockSpec((tj, lay, width), lambda j: (j, 0, 0)),
        ],
        out_specs=pl.BlockSpec((tj, lay, width), lambda j: (j, 0, 0)),
        out_shape=jax.ShapeDtypeStruct((feats, lay, width), jnp.bfloat16),
        cost_estimate=cost,
    )(lhs_int, rhs_st, h_int, wd)


def per_device(activations, enc_weight, dec_weight, enc_bias, n_layer, n_feat):
    nb, rloc, lay, width = activations.shape
    feats = enc_weight.shape[2]
    lw = lay * width
    rows = rloc * n_feat
    cst = 2.0 / rows
    pen = penalty / rows
    c1 = rate * cst

    xn = normalize(activations).reshape(nb, rloc, lw)
    xg = allgather_rows(xn, "feat", n_feat)
    x0, x1 = xg[0], xg[1]
    x0f = x0.astype(jnp.float32)
    x1f = x1.astype(jnp.float32)

    we_flat = enc_weight.reshape(lw, feats)
    wd_flat = dec_weight.reshape(feats, lw)

    pre_part = jnp.dot(xg.reshape(nb * rows, lw), we_flat, preferred_element_type=jnp.float32)
    gram = lax.dot_general(x1, x0, (((1,), (1,)), ((), ())), preferred_element_type=jnp.float32)
    gk = -(-(rows * rows) // feats)
    gpad = jnp.pad(gram.reshape(-1), (0, gk * feats - rows * rows)).reshape(gk, feats)
    red1 = allreduce(jnp.concatenate([pre_part[:rows], gpad], axis=0), "layer", n_layer)
    pre_x0 = red1[:rows]
    gram10 = red1[rows:].reshape(-1)[: rows * rows].reshape(rows, rows)
    pre_x1 = allreduce(pre_part[rows:], "layer", n_layer)

    sq0 = jnp.stack(
        [jnp.sum(jnp.square(wd_flat[:, l * width : (l + 1) * width].astype(jnp.float32)), axis=1) for l in range(lay)],
        axis=1,
    )
    lens0 = jnp.sqrt(sq0 + eps)

    pre0 = pre_x0 + enc_bias
    pos0 = jnp.maximum(pre0, 0.0)
    act0 = pos0 * pos0
    actb0 = act0.astype(jnp.bfloat16)
    asum0 = jnp.sum(act0, axis=0)
    rec0 = allreduce(jnp.dot(actb0, wd_flat, preferred_element_type=jnp.float32), "feat", n_feat)
    errb0 = (rec0 - x0f).astype(jnp.bfloat16)
    d0 = per_layer_dot(errb0, wd_flat, lay, width)
    dact0_part = cst * jnp.sum(d0, axis=0) + pen * jnp.sum(lens0, axis=1)[None, :]
    dact0 = allreduce(dact0_part, "layer", n_layer)
    dpre0 = dact0 * 2.0 * pos0
    dpreb0 = dpre0.astype(jnp.bfloat16)
    gbe0 = jnp.sum(dpre0, axis=0)

    delta0 = -rate * pen * asum0[:, None] / lens0
    s0 = 1.0 + delta0
    be1 = enc_bias - rate * gbe0
    corr = jnp.dot(gram10, dpreb0.astype(jnp.float32), precision=HI)
    pre1 = pre_x1 - rate * corr + be1
    pos1 = jnp.maximum(pre1, 0.0)
    act1 = pos1 * pos1
    actb1 = act1.astype(jnp.bfloat16)
    asum1 = jnp.sum(act1, axis=0)
    actb0f = actb0.astype(jnp.float32)
    actb1f = actb1.astype(jnp.float32)
    h10 = jnp.dot(actb1f, actb0f.T, precision=HI)
    rec1_part = rec1_dot(actb1, delta0, wd_flat, lay, width) - c1 * jnp.dot(h10, errb0.astype(jnp.float32), precision=HI)
    rec1 = allreduce(rec1_part, "feat", n_feat)
    errb1 = (rec1 - x1f).astype(jnp.bfloat16)

    e0f = errb0.astype(jnp.float32).reshape(rows, lay, width)
    e1f = errb1.astype(jnp.float32).reshape(rows, lay, width)
    g00 = jnp.einsum("rld,sld->lrs", e0f, e0f, precision=HI)
    g10 = jnp.einsum("rld,sld->lrs", e1f, e0f, precision=HI)
    cross = jnp.einsum("rj,lrj->jl", actb0f, d0, precision=HI)
    quad = jnp.einsum("rj,lrs,sj->jl", actb0f, g00, actb0f, precision=HI)
    sq1 = s0 * s0 * sq0 - 2.0 * c1 * s0 * cross + c1 * c1 * quad
    lens1 = jnp.sqrt(jnp.maximum(sq1, 0.0) + eps)

    d1 = per_layer_dot(errb1, wd_flat, lay, width)
    lowr = jnp.einsum("lrs,sj->lrj", g10, actb0f, precision=HI)
    dd1 = s0.T[:, None, :] * d1 - c1 * lowr
    dact1_part = cst * jnp.sum(dd1, axis=0) + pen * jnp.sum(lens1, axis=1)[None, :]

    g0 = cst - pen * c1 * asum1[:, None] / lens1
    hcoef = pen * (asum0[:, None] / lens0 + asum1[:, None] * s0 / lens1)
    lhs0 = g0.T[:, :, None] * actb0f.T[None, :, :]
    hi0, lo0 = split_bf16(lhs0)
    lhs1 = jnp.broadcast_to((cst * actb1f).T.astype(jnp.bfloat16)[None], (lay, feats, rows))
    lhs = jnp.concatenate([lhs1, hi0, lo0], axis=2)
    rhs = jnp.concatenate([errb1, errb0, errb0], axis=0)
    rhs3 = rhs.reshape(3 * rows, lay, width).transpose(1, 0, 2)
    dact1_part, lhs, rhs3, hcoef = lax.optimization_barrier((dact1_part, lhs, rhs3, hcoef))
    dec_step = dec_call(lhs, rhs3, hcoef, dec_weight)
    dact1 = allreduce(dact1_part, "layer", n_layer)
    dact1, dec_step = lax.optimization_barrier((dact1, dec_step))
    dpre1 = dact1 * 2.0 * pos1
    dpreb1 = dpre1.astype(jnp.bfloat16)
    gbe1 = jnp.sum(dpre1, axis=0)

    dp = jnp.concatenate([dpreb0, dpreb1], axis=0)
    enc = lax.dot_general(xg.reshape(nb * rows, lw), dp, (((0,), (0,)), ((), ())), preferred_element_type=jnp.float32)
    enc_step = enc.astype(jnp.bfloat16).reshape(lay, width, feats)
    bias_step = gbe0 + gbe1
    return (enc_step, dec_step, bias_step)


def solution(mesh):
    n_layer = mesh.shape["layer"]
    n_feat = mesh.shape["feat"]
    in_specs = (
        P(None, "feat", "layer", None),
        P("layer", None, "feat"),
        P("feat", "layer", None),
        P("feat"),
    )
    out_specs = (P("layer", None, "feat"), P("feat", "layer", None), P("feat"))

    def body(a, we, wd, be):
        return per_device(a, we, wd, be, n_layer, n_feat)

    return jax.shard_map(body, mesh=mesh, in_specs=in_specs, out_specs=out_specs, check_vma=False)
```

```python
import jax
import jax.numpy as jnp
from jax import lax
from jax.experimental import pallas as pl
from jax.sharding import PartitionSpec as P

rate = 0.01
penalty = 2.0
eps = 1e-06
HI = lax.Precision.HIGHEST


def normalize(x):
    xf = x.astype(jnp.float32)
    scale = jnp.sqrt(jnp.mean(xf * xf, axis=-1, keepdims=True) + eps)
    return (xf / scale).astype(jnp.bfloat16)


def allreduce(x, axis, n):
    k = 1
    while k < n:
        x = x + lax.ppermute(x, axis, [(i, i ^ k) for i in range(n)])
        k *= 2
    return x


def allgather_rows(x, axis, n):
    me = lax.axis_index(axis)
    k = 1
    while k < n:
        got = lax.ppermute(x, axis, [(i, i ^ k) for i in range(n)])
        low = (me // k) % 2 == 0
        x = jnp.where(low, jnp.concatenate([x, got], axis=1), jnp.concatenate([got, x], axis=1))
        k *= 2
    return x


def split_bf16(v):
    hi = v.astype(jnp.bfloat16)
    lo = (v - hi.astype(jnp.float32)).astype(jnp.bfloat16)
    return hi, lo


def block_rows(e, lay, width):
    rows = e.shape[0]
    e3 = e.reshape(rows, lay, width)
    eye = jnp.eye(lay, dtype=e.dtype)
    blk = eye[:, None, :, None] * e3[None, :, :, :]
    return blk.reshape(lay * rows, lay * width)


def per_layer_dot(e, wd2, lay, width):
    rows = e.shape[0]
    blk = block_rows(e, lay, width)
    out = lax.dot_general(wd2, blk, (((1,), (1,)), ((), ())), preferred_element_type=jnp.float32)
    return out.reshape(wd2.shape[0], lay, rows).transpose(1, 2, 0)


def rec1_dot(actb1, delta, wd2, lay, width):
    rows = actb1.shape[0]
    corr = [(actb1.astype(jnp.float32) * delta[:, l][None, :]).astype(jnp.bfloat16) for l in range(lay)]
    lhs = jnp.concatenate([actb1] + corr, axis=0)
    out = jnp.dot(lhs, wd2, preferred_element_type=jnp.float32)
    parts = []
    for l in range(lay):
        cols = slice(l * width, (l + 1) * width)
        parts.append(out[:rows, cols] + out[(l + 1) * rows : (l + 2) * rows, cols])
    return jnp.concatenate(parts, axis=1)


def dec_kernel(lhs_ref, rhs_ref, h_ref, wd_ref, out_ref):
    tj, lay, width = wd_ref.shape
    acc = jnp.dot(lhs_ref[...], rhs_ref[...], preferred_element_type=jnp.float32)
    w = wd_ref[...].reshape(tj * lay, width).astype(jnp.float32)
    acc = acc + h_ref[...] * w
    out_ref[...] = acc.astype(out_ref.dtype).reshape(tj, lay, width)


def dec_prep(lhs, hcoef):
    lay, feats, k = lhs.shape
    eye = jnp.eye(lay, dtype=lhs.dtype)
    lhs_int = (eye[None, :, :, None] * lhs.transpose(1, 0, 2)[:, :, None, :]).reshape(feats * lay, lay * k)
    h_int = hcoef.reshape(feats * lay, 1)
    return lhs_int, h_int


def dec_kernel_acc(lhs_ref, rhs_ref, h_ref, wd_ref, prev_ref, out_ref):
    del prev_ref
    dec_kernel(lhs_ref, rhs_ref, h_ref, wd_ref, out_ref)


def dec_call(lhs_int, rhs_st, h_int, wd, part, parts, prev=None):
    feats, lay, width = wd.shape
    k2 = lhs_int.shape[1]
    tj = min(256, feats // parts)
    steps = feats // parts // tj
    off = part * steps
    cost = pl.CostEstimate(
        flops=2 * feats * lay * width * k2 // parts, transcendentals=0, bytes_accessed=4 * feats * lay * width // parts
    )
    in_specs = [
        pl.BlockSpec((tj * lay, k2), lambda j: (j + off, 0)),
        pl.BlockSpec((k2, width), lambda j: (0, 0)),
        pl.BlockSpec((tj * lay, 1), lambda j: (j + off, 0)),
        pl.BlockSpec((tj, lay, width), lambda j: (j + off, 0, 0)),
    ]
    args = [lhs_int, rhs_st, h_int, wd]
    kern, aliases = dec_kernel, {}
    if prev is not None:
        in_specs.append(pl.BlockSpec(memory_space=pl.ANY))
        args.append(prev)
        kern, aliases = dec_kernel_acc, {4: 0}
    return pl.pallas_call(
        kern,
        grid=(steps,),
        in_specs=in_specs,
        out_specs=pl.BlockSpec((tj, lay, width), lambda j: (j + off, 0, 0)),
        out_shape=jax.ShapeDtypeStruct((feats, lay, width), jnp.bfloat16),
        input_output_aliases=aliases,
        cost_estimate=cost,
    )(*args)


def per_device(activations, enc_weight, dec_weight, enc_bias, n_layer, n_feat):
    nb, rloc, lay, width = activations.shape
    feats = enc_weight.shape[2]
    lw = lay * width
    rows = rloc * n_feat
    cst = 2.0 / rows
    pen = penalty / rows
    c1 = rate * cst

    xn = normalize(activations).reshape(nb, rloc, lw)
    xg = allgather_rows(xn, "feat", n_feat)
    x0, x1 = xg[0], xg[1]
    x0f = x0.astype(jnp.float32)
    x1f = x1.astype(jnp.float32)

    we_flat = enc_weight.reshape(lw, feats)
    wd_flat = dec_weight.reshape(feats, lw)

    pre_part = jnp.dot(xg.reshape(nb * rows, lw), we_flat, preferred_element_type=jnp.float32)
    gram = lax.dot_general(x1, x0, (((1,), (1,)), ((), ())), preferred_element_type=jnp.float32)
    gk = -(-(rows * rows) // feats)
    gpad = jnp.pad(gram.reshape(-1), (0, gk * feats - rows * rows)).reshape(gk, feats)
    red1 = allreduce(jnp.concatenate([pre_part[:rows], gpad], axis=0), "layer", n_layer)
    pre_x0 = red1[:rows]
    gram10 = red1[rows:].reshape(-1)[: rows * rows].reshape(rows, rows)
    pre_x1_part = pre_part[rows:]

    sq0 = jnp.stack(
        [jnp.sum(jnp.square(wd_flat[:, l * width : (l + 1) * width].astype(jnp.float32)), axis=1) for l in range(lay)],
        axis=1,
    )
    lens0 = jnp.sqrt(sq0 + eps)

    pre0 = pre_x0 + enc_bias
    pos0 = jnp.maximum(pre0, 0.0)
    act0 = pos0 * pos0
    actb0 = act0.astype(jnp.bfloat16)
    asum0 = jnp.sum(act0, axis=0)
    rec0 = allreduce(jnp.dot(actb0, wd_flat, preferred_element_type=jnp.float32), "feat", n_feat)
    errb0 = (rec0 - x0f).astype(jnp.bfloat16)
    pre_x1_part, errb0 = lax.optimization_barrier((pre_x1_part, errb0))
    pre_x1 = allreduce(pre_x1_part, "layer", n_layer)
    d0 = per_layer_dot(errb0, wd_flat, lay, width)
    dact0_part = cst * jnp.sum(d0, axis=0) + pen * jnp.sum(lens0, axis=1)[None, :]
    dact0 = allreduce(dact0_part, "layer", n_layer)
    dpre0 = dact0 * 2.0 * pos0
    dpreb0 = dpre0.astype(jnp.bfloat16)
    gbe0 = jnp.sum(dpre0, axis=0)

    delta0 = -rate * pen * asum0[:, None] / lens0
    s0 = 1.0 + delta0
    be1 = enc_bias - rate * gbe0
    corr = jnp.dot(gram10, dpreb0.astype(jnp.float32), precision=HI)
    pre1 = pre_x1 - rate * corr + be1
    pos1 = jnp.maximum(pre1, 0.0)
    act1 = pos1 * pos1
    actb1 = act1.astype(jnp.bfloat16)
    asum1 = jnp.sum(act1, axis=0)
    actb0f = actb0.astype(jnp.float32)
    actb1f = actb1.astype(jnp.float32)
    h10 = jnp.dot(actb1f, actb0f.T, precision=HI)
    rec1_part = rec1_dot(actb1, delta0, wd_flat, lay, width) - c1 * jnp.dot(h10, errb0.astype(jnp.float32), precision=HI)
    rec1 = allreduce(rec1_part, "feat", n_feat)
    errb1 = (rec1 - x1f).astype(jnp.bfloat16)

    e0f = errb0.astype(jnp.float32).reshape(rows, lay, width)
    e1f = errb1.astype(jnp.float32).reshape(rows, lay, width)
    g00 = jnp.einsum("rld,sld->lrs", e0f, e0f, precision=HI)
    g10 = jnp.einsum("rld,sld->lrs", e1f, e0f, precision=HI)
    cross = jnp.einsum("rj,lrj->jl", actb0f, d0, precision=HI)
    quad = jnp.einsum("rj,lrs,sj->jl", actb0f, g00, actb0f, precision=HI)
    sq1 = s0 * s0 * sq0 - 2.0 * c1 * s0 * cross + c1 * c1 * quad
    lens1 = jnp.sqrt(jnp.maximum(sq1, 0.0) + eps)

    d1 = per_layer_dot(errb1, wd_flat, lay, width)
    lowr = jnp.einsum("lrs,sj->lrj", g10, actb0f, precision=HI)
    dd1 = s0.T[:, None, :] * d1 - c1 * lowr
    dact1_part = cst * jnp.sum(dd1, axis=0) + pen * jnp.sum(lens1, axis=1)[None, :]

    g0 = cst - pen * c1 * asum1[:, None] / lens1
    hcoef = pen * (asum0[:, None] / lens0 + asum1[:, None] * s0 / lens1)
    lhs0 = g0.T[:, :, None] * actb0f.T[None, :, :]
    hi0, lo0 = split_bf16(lhs0)
    lhs1 = jnp.broadcast_to((cst * actb1f).T.astype(jnp.bfloat16)[None], (lay, feats, rows))
    lhs = jnp.concatenate([lhs1, hi0, lo0], axis=2)
    lhs_int, h_int = dec_prep(lhs, hcoef)
    rhs = jnp.concatenate([errb1, errb0, errb0], axis=0)
    rhs_st = rhs.reshape(3 * rows, lay, width).transpose(1, 0, 2).reshape(lay * 3 * rows, width)
    x = dact1_part
    dec_step = None
    k = 1
    part = 0
    while k < n_layer:
        x, lhs_int, rhs_st, h_int = lax.optimization_barrier((x, lhs_int, rhs_st, h_int))
        got = lax.ppermute(x, "layer", [(i, i ^ k) for i in range(n_layer)])
        if part < 2:
            dec_step = dec_call(lhs_int, rhs_st, h_int, dec_weight, part, 2, dec_step)
            part += 1
        x = x + got
        x, dec_step = lax.optimization_barrier((x, dec_step))
        k *= 2
    while part < 2:
        dec_step = dec_call(lhs_int, rhs_st, h_int, dec_weight, part, 2, dec_step)
        part += 1
    dact1 = x

    dpre1 = dact1 * 2.0 * pos1
    dpreb1 = dpre1.astype(jnp.bfloat16)
    gbe1 = jnp.sum(dpre1, axis=0)

    dp = jnp.concatenate([dpreb0, dpreb1], axis=0)
    enc = lax.dot_general(xg.reshape(nb * rows, lw), dp, (((0,), (0,)), ((), ())), preferred_element_type=jnp.float32)
    enc_step = enc.astype(jnp.bfloat16).reshape(lay, width, feats)
    bias_step = gbe0 + gbe1
    return (enc_step, dec_step, bias_step)


def solution(mesh):
    n_layer = mesh.shape["layer"]
    n_feat = mesh.shape["feat"]
    in_specs = (
        P(None, "feat", "layer", None),
        P("layer", None, "feat"),
        P("feat", "layer", None),
        P("feat"),
    )
    out_specs = (P("layer", None, "feat"), P("feat", "layer", None), P("feat"))

    def body(a, we, wd, be):
        return per_device(a, we, wd, be, n_layer, n_feat)

    return jax.shard_map(body, mesh=mesh, in_specs=in_specs, out_specs=out_specs, check_vma=False)
```

```python
import jax
import jax.numpy as jnp
from jax import lax
from jax.experimental import pallas as pl
from jax.sharding import PartitionSpec as P

rate = 0.01
penalty = 2.0
eps = 1e-06
HI = lax.Precision.HIGHEST


def normalize(x):
    xf = x.astype(jnp.float32)
    scale = jnp.sqrt(jnp.mean(xf * xf, axis=-1, keepdims=True) + eps)
    return (xf / scale).astype(jnp.bfloat16)


def allreduce(x, axis, n):
    k = 1
    while k < n:
        x = x + lax.ppermute(x, axis, [(i, i ^ k) for i in range(n)])
        k *= 2
    return x


def allgather_rows(x, axis, n):
    me = lax.axis_index(axis)
    k = 1
    while k < n:
        got = lax.ppermute(x, axis, [(i, i ^ k) for i in range(n)])
        low = (me // k) % 2 == 0
        x = jnp.where(low, jnp.concatenate([x, got], axis=1), jnp.concatenate([got, x], axis=1))
        k *= 2
    return x


def split_bf16(v):
    hi = v.astype(jnp.bfloat16)
    lo = (v - hi.astype(jnp.float32)).astype(jnp.bfloat16)
    return hi, lo


def block_rows(e, lay, width):
    rows = e.shape[0]
    e3 = e.reshape(rows, lay, width)
    eye = jnp.eye(lay, dtype=e.dtype)
    blk = eye[:, None, :, None] * e3[None, :, :, :]
    return blk.reshape(lay * rows, lay * width)


def per_layer_dot(e, wd2, lay, width):
    outs = []
    for l in range(lay):
        cols = slice(l * width, (l + 1) * width)
        outs.append(lax.dot_general(wd2[:, cols], e[:, cols], (((1,), (1,)), ((), ())), preferred_element_type=jnp.float32))
    return jnp.stack(outs, axis=0).transpose(0, 2, 1)


def rec1_dot(actb1, delta, wd2, lay, width):
    rows = actb1.shape[0]
    parts = []
    for l in range(lay):
        cols = slice(l * width, (l + 1) * width)
        corr = (actb1.astype(jnp.float32) * delta[:, l][None, :]).astype(jnp.bfloat16)
        out = jnp.dot(jnp.concatenate([actb1, corr], axis=0), wd2[:, cols], preferred_element_type=jnp.float32)
        parts.append(out[:rows] + out[rows:])
    return jnp.concatenate(parts, axis=1)


def dec_kernel(lhs_ref, rhs_ref, h_ref, wd_ref, out_ref):
    tj, lay, width = wd_ref.shape
    acc = jnp.dot(lhs_ref[...], rhs_ref[...], preferred_element_type=jnp.float32)
    w = wd_ref[...].reshape(tj * lay, width).astype(jnp.float32)
    acc = acc + h_ref[...] * w
    out_ref[...] = acc.astype(out_ref.dtype).reshape(tj, lay, width)


def dec_prep(lhs, hcoef):
    lay, feats, k = lhs.shape
    eye = jnp.eye(lay, dtype=lhs.dtype)
    lhs_int = (eye[None, :, :, None] * lhs.transpose(1, 0, 2)[:, :, None, :]).reshape(feats * lay, lay * k)
    h_int = hcoef.reshape(feats * lay, 1)
    return lhs_int, h_int


def dec_kernel_acc(lhs_ref, rhs_ref, h_ref, wd_ref, prev_ref, out_ref):
    del prev_ref
    dec_kernel(lhs_ref, rhs_ref, h_ref, wd_ref, out_ref)


def dec_call(lhs_int, rhs_st, h_int, wd, part, parts, prev=None):
    feats, lay, width = wd.shape
    k2 = lhs_int.shape[1]
    tj = min(256, feats // parts)
    steps = feats // parts // tj
    off = part * steps
    cost = pl.CostEstimate(
        flops=2 * feats * lay * width * k2 // parts, transcendentals=0, bytes_accessed=4 * feats * lay * width // parts
    )
    in_specs = [
        pl.BlockSpec((tj * lay, k2), lambda j: (j + off, 0)),
        pl.BlockSpec((k2, width), lambda j: (0, 0)),
        pl.BlockSpec((tj * lay, 1), lambda j: (j + off, 0)),
        pl.BlockSpec((tj, lay, width), lambda j: (j + off, 0, 0)),
    ]
    args = [lhs_int, rhs_st, h_int, wd]
    kern, aliases = dec_kernel, {}
    if prev is not None:
        in_specs.append(pl.BlockSpec(memory_space=pl.ANY))
        args.append(prev)
        kern, aliases = dec_kernel_acc, {4: 0}
    return pl.pallas_call(
        kern,
        grid=(steps,),
        in_specs=in_specs,
        out_specs=pl.BlockSpec((tj, lay, width), lambda j: (j + off, 0, 0)),
        out_shape=jax.ShapeDtypeStruct((feats, lay, width), jnp.bfloat16),
        input_output_aliases=aliases,
        cost_estimate=cost,
    )(*args)


def per_device(activations, enc_weight, dec_weight, enc_bias, n_layer, n_feat):
    nb, rloc, lay, width = activations.shape
    feats = enc_weight.shape[2]
    lw = lay * width
    rows = rloc * n_feat
    cst = 2.0 / rows
    pen = penalty / rows
    c1 = rate * cst

    xn = normalize(activations).reshape(nb, rloc, lw)
    xg = allgather_rows(xn, "feat", n_feat)
    x0, x1 = xg[0], xg[1]
    x0f = x0.astype(jnp.float32)
    x1f = x1.astype(jnp.float32)

    we_flat = enc_weight.reshape(lw, feats)
    wd_flat = dec_weight.reshape(feats, lw)

    pre_part = jnp.dot(xg.reshape(nb * rows, lw), we_flat, preferred_element_type=jnp.float32)
    gram = lax.dot_general(x1, x0, (((1,), (1,)), ((), ())), preferred_element_type=jnp.float32)
    gk = -(-(rows * rows) // feats)
    gpad = jnp.pad(gram.reshape(-1), (0, gk * feats - rows * rows)).reshape(gk, feats)
    red1 = allreduce(jnp.concatenate([pre_part[:rows], gpad], axis=0), "layer", n_layer)
    pre_x0 = red1[:rows]
    gram10 = red1[rows:].reshape(-1)[: rows * rows].reshape(rows, rows)
    pre_x1_part = pre_part[rows:]

    sq0 = jnp.stack(
        [jnp.sum(jnp.square(wd_flat[:, l * width : (l + 1) * width].astype(jnp.float32)), axis=1) for l in range(lay)],
        axis=1,
    )
    lens0 = jnp.sqrt(sq0 + eps)

    pre0 = pre_x0 + enc_bias
    pos0 = jnp.maximum(pre0, 0.0)
    act0 = pos0 * pos0
    actb0 = act0.astype(jnp.bfloat16)
    asum0 = jnp.sum(act0, axis=0)
    rec0 = allreduce(jnp.dot(actb0, wd_flat, preferred_element_type=jnp.float32), "feat", n_feat)
    errb0 = (rec0 - x0f).astype(jnp.bfloat16)
    d0 = per_layer_dot(errb0, wd_flat, lay, width)
    dact0_part = cst * jnp.sum(d0, axis=0) + pen * jnp.sum(lens0, axis=1)[None, :]
    red3 = allreduce(jnp.concatenate([dact0_part, pre_x1_part], axis=0), "layer", n_layer)
    dact0 = red3[:rows]
    pre_x1 = red3[rows:]
    dpre0 = dact0 * 2.0 * pos0
    dpreb0 = dpre0.astype(jnp.bfloat16)
    gbe0 = jnp.sum(dpre0, axis=0)

    delta0 = -rate * pen * asum0[:, None] / lens0
    s0 = 1.0 + delta0
    be1 = enc_bias - rate * gbe0
    corr = jnp.dot(gram10, dpreb0.astype(jnp.float32), precision=HI)
    pre1 = pre_x1 - rate * corr + be1
    pos1 = jnp.maximum(pre1, 0.0)
    act1 = pos1 * pos1
    actb1 = act1.astype(jnp.bfloat16)
    asum1 = jnp.sum(act1, axis=0)
    actb0f = actb0.astype(jnp.float32)
    actb1f = actb1.astype(jnp.float32)
    h10 = jnp.dot(actb1f, actb0f.T, precision=HI)
    rec1_part = rec1_dot(actb1, delta0, wd_flat, lay, width) - c1 * jnp.dot(h10, errb0.astype(jnp.float32), precision=HI)
    rec1 = allreduce(rec1_part, "feat", n_feat)
    errb1 = (rec1 - x1f).astype(jnp.bfloat16)

    e0f = errb0.astype(jnp.float32).reshape(rows, lay, width)
    e1f = errb1.astype(jnp.float32).reshape(rows, lay, width)
    g00 = jnp.einsum("rld,sld->lrs", e0f, e0f, precision=HI)
    g10 = jnp.einsum("rld,sld->lrs", e1f, e0f, precision=HI)
    cross = jnp.einsum("rj,lrj->jl", actb0f, d0, precision=HI)
    quad = jnp.einsum("rj,lrs,sj->jl", actb0f, g00, actb0f, precision=HI)
    sq1 = s0 * s0 * sq0 - 2.0 * c1 * s0 * cross + c1 * c1 * quad
    lens1 = jnp.sqrt(jnp.maximum(sq1, 0.0) + eps)

    d1 = per_layer_dot(errb1, wd_flat, lay, width)
    lowr = jnp.einsum("lrs,sj->lrj", g10, actb0f, precision=HI)
    dd1 = s0.T[:, None, :] * d1 - c1 * lowr
    dact1_part = cst * jnp.sum(dd1, axis=0) + pen * jnp.sum(lens1, axis=1)[None, :]

    g0 = cst - pen * c1 * asum1[:, None] / lens1
    hcoef = pen * (asum0[:, None] / lens0 + asum1[:, None] * s0 / lens1)
    lhs0 = g0.T[:, :, None] * actb0f.T[None, :, :]
    hi0, lo0 = split_bf16(lhs0)
    lhs1 = jnp.broadcast_to((cst * actb1f).T.astype(jnp.bfloat16)[None], (lay, feats, rows))
    lhs = jnp.concatenate([lhs1, hi0, lo0], axis=2)
    lhs_int, h_int = dec_prep(lhs, hcoef)
    rhs = jnp.concatenate([errb1, errb0, errb0], axis=0)
    rhs_st = rhs.reshape(3 * rows, lay, width).transpose(1, 0, 2).reshape(lay * 3 * rows, width)
    x = dact1_part
    dec_step = None
    k = 1
    part = 0
    while k < n_layer:
        x, lhs_int, rhs_st, h_int = lax.optimization_barrier((x, lhs_int, rhs_st, h_int))
        got = lax.ppermute(x, "layer", [(i, i ^ k) for i in range(n_layer)])
        if part < 2:
            dec_step = dec_call(lhs_int, rhs_st, h_int, dec_weight, part, 2, dec_step)
            part += 1
        x = x + got
        x, dec_step = lax.optimization_barrier((x, dec_step))
        k *= 2
    while part < 2:
        dec_step = dec_call(lhs_int, rhs_st, h_int, dec_weight, part, 2, dec_step)
        part += 1
    dact1 = x

    dpre1 = dact1 * 2.0 * pos1
    dpreb1 = dpre1.astype(jnp.bfloat16)
    gbe1 = jnp.sum(dpre1, axis=0)

    dp = jnp.concatenate([dpreb0, dpreb1], axis=0)
    enc = lax.dot_general(xg.reshape(nb * rows, lw), dp, (((0,), (0,)), ((), ())), preferred_element_type=jnp.float32)
    enc_step = enc.astype(jnp.bfloat16).reshape(lay, width, feats)
    bias_step = gbe0 + gbe1
    return (enc_step, dec_step, bias_step)


def solution(mesh):
    n_layer = mesh.shape["layer"]
    n_feat = mesh.shape["feat"]
    in_specs = (
        P(None, "feat", "layer", None),
        P("layer", None, "feat"),
        P("feat", "layer", None),
        P("feat"),
    )
    out_specs = (P("layer", None, "feat"), P("feat", "layer", None), P("feat"))

    def body(a, we, wd, be):
        return per_device(a, we, wd, be, n_layer, n_feat)

    return jax.shard_map(body, mesh=mesh, in_specs=in_specs, out_specs=out_specs, check_vma=False)
```

```python
import jax
import jax.numpy as jnp
from jax import lax
from jax.experimental import pallas as pl
from jax.sharding import PartitionSpec as P

rate = 0.01
penalty = 2.0
eps = 1e-06
HI = lax.Precision.HIGHEST


def normalize(x):
    xf = x.astype(jnp.float32)
    scale = jnp.sqrt(jnp.mean(xf * xf, axis=-1, keepdims=True) + eps)
    return (xf / scale).astype(jnp.bfloat16)


def allreduce(x, axis, n):
    k = 1
    while k < n:
        x = x + lax.ppermute(x, axis, [(i, i ^ k) for i in range(n)])
        k *= 2
    return x


def allgather_rows(x, axis, n):
    me = lax.axis_index(axis)
    k = 1
    while k < n:
        got = lax.ppermute(x, axis, [(i, i ^ k) for i in range(n)])
        low = (me // k) % 2 == 0
        x = jnp.where(low, jnp.concatenate([x, got], axis=1), jnp.concatenate([got, x], axis=1))
        k *= 2
    return x


def split_bf16(v):
    hi = v.astype(jnp.bfloat16)
    lo = (v - hi.astype(jnp.float32)).astype(jnp.bfloat16)
    return hi, lo


def block_rows(e, lay, width):
    rows = e.shape[0]
    e3 = e.reshape(rows, lay, width)
    eye = jnp.eye(lay, dtype=e.dtype)
    blk = eye[:, None, :, None] * e3[None, :, :, :]
    return blk.reshape(lay * rows, lay * width)


def per_layer_dot(e, wd2, lay, width):
    rows = e.shape[0]
    blk = block_rows(e, lay, width)
    out = lax.dot_general(wd2, blk, (((1,), (1,)), ((), ())), preferred_element_type=jnp.float32)
    return out.reshape(wd2.shape[0], lay, rows).transpose(1, 2, 0)


def rec1_dot(actb1, delta, wd2, lay, width):
    rows = actb1.shape[0]
    parts = []
    for l in range(lay):
        cols = slice(l * width, (l + 1) * width)
        corr = (actb1.astype(jnp.float32) * delta[:, l][None, :]).astype(jnp.bfloat16)
        out = jnp.dot(jnp.concatenate([actb1, corr], axis=0), wd2[:, cols], preferred_element_type=jnp.float32)
        parts.append(out[:rows] + out[rows:])
    return jnp.concatenate(parts, axis=1)


def dec_kernel(lhs_ref, rhs_ref, h_ref, wd_ref, out_ref):
    tj, lay, width = wd_ref.shape
    acc = jnp.dot(lhs_ref[...], rhs_ref[...], preferred_element_type=jnp.float32)
    w = wd_ref[...].reshape(tj * lay, width).astype(jnp.float32)
    acc = acc + h_ref[...] * w
    out_ref[...] = acc.astype(out_ref.dtype).reshape(tj, lay, width)


def dec_prep(lhs, hcoef):
    lay, feats, k = lhs.shape
    eye = jnp.eye(lay, dtype=lhs.dtype)
    lhs_int = (eye[None, :, :, None] * lhs.transpose(1, 0, 2)[:, :, None, :]).reshape(feats * lay, lay * k)
    h_int = hcoef.reshape(feats * lay, 1)
    return lhs_int, h_int


def dec_kernel_acc(lhs_ref, rhs_ref, h_ref, wd_ref, prev_ref, out_ref):
    del prev_ref
    dec_kernel(lhs_ref, rhs_ref, h_ref, wd_ref, out_ref)


def dec_call(lhs_int, rhs_st, h_int, wd, part, parts, prev=None):
    feats, lay, width = wd.shape
    k2 = lhs_int.shape[1]
    tj = min(256, feats // parts)
    steps = feats // parts // tj
    off = part * steps
    cost = pl.CostEstimate(
        flops=2 * feats * lay * width * k2 // parts, transcendentals=0, bytes_accessed=4 * feats * lay * width // parts
    )
    in_specs = [
        pl.BlockSpec((tj * lay, k2), lambda j: (j + off, 0)),
        pl.BlockSpec((k2, width), lambda j: (0, 0)),
        pl.BlockSpec((tj * lay, 1), lambda j: (j + off, 0)),
        pl.BlockSpec((tj, lay, width), lambda j: (j + off, 0, 0)),
    ]
    args = [lhs_int, rhs_st, h_int, wd]
    kern, aliases = dec_kernel, {}
    if prev is not None:
        in_specs.append(pl.BlockSpec(memory_space=pl.ANY))
        args.append(prev)
        kern, aliases = dec_kernel_acc, {4: 0}
    return pl.pallas_call(
        kern,
        grid=(steps,),
        in_specs=in_specs,
        out_specs=pl.BlockSpec((tj, lay, width), lambda j: (j + off, 0, 0)),
        out_shape=jax.ShapeDtypeStruct((feats, lay, width), jnp.bfloat16),
        input_output_aliases=aliases,
        cost_estimate=cost,
    )(*args)


def per_device(activations, enc_weight, dec_weight, enc_bias, n_layer, n_feat):
    nb, rloc, lay, width = activations.shape
    feats = enc_weight.shape[2]
    lw = lay * width
    rows = rloc * n_feat
    cst = 2.0 / rows
    pen = penalty / rows
    c1 = rate * cst

    xn = normalize(activations).reshape(nb, rloc, lw)
    xg = allgather_rows(xn, "feat", n_feat)
    x0, x1 = xg[0], xg[1]
    x0f = x0.astype(jnp.float32)
    x1f = x1.astype(jnp.float32)

    we_flat = enc_weight.reshape(lw, feats)
    wd_flat = dec_weight.reshape(feats, lw)

    pre_part = jnp.dot(xg.reshape(nb * rows, lw), we_flat, preferred_element_type=jnp.float32)
    gram = lax.dot_general(x1, x0, (((1,), (1,)), ((), ())), preferred_element_type=jnp.float32)
    gk = -(-(rows * rows) // feats)
    gpad = jnp.pad(gram.reshape(-1), (0, gk * feats - rows * rows)).reshape(gk, feats)
    red1 = allreduce(jnp.concatenate([pre_part[:rows], gpad], axis=0), "layer", n_layer)
    pre_x0 = red1[:rows]
    gram10 = red1[rows:].reshape(-1)[: rows * rows].reshape(rows, rows)
    pre_x1_part = pre_part[rows:]

    sq0 = jnp.stack(
        [jnp.sum(jnp.square(wd_flat[:, l * width : (l + 1) * width].astype(jnp.float32)), axis=1) for l in range(lay)],
        axis=1,
    )
    lens0 = jnp.sqrt(sq0 + eps)

    pre0 = pre_x0 + enc_bias
    pos0 = jnp.maximum(pre0, 0.0)
    act0 = pos0 * pos0
    actb0 = act0.astype(jnp.bfloat16)
    asum0 = jnp.sum(act0, axis=0)
    rec0_part = jnp.dot(actb0, wd_flat, preferred_element_type=jnp.float32)
    pre_x1_part, rec0_part = lax.optimization_barrier((pre_x1_part, rec0_part))
    pre_x1 = allreduce(pre_x1_part, "layer", n_layer)
    rec0 = allreduce(rec0_part, "feat", n_feat)
    errb0 = (rec0 - x0f).astype(jnp.bfloat16)
    d0 = per_layer_dot(errb0, wd_flat, lay, width)
    dact0_part = cst * jnp.sum(d0, axis=0) + pen * jnp.sum(lens0, axis=1)[None, :]
    dact0 = allreduce(dact0_part, "layer", n_layer)
    dpre0 = dact0 * 2.0 * pos0
    dpreb0 = dpre0.astype(jnp.bfloat16)
    gbe0 = jnp.sum(dpre0, axis=0)

    delta0 = -rate * pen * asum0[:, None] / lens0
    s0 = 1.0 + delta0
    be1 = enc_bias - rate * gbe0
    corr = jnp.dot(gram10, dpreb0.astype(jnp.float32), precision=HI)
    pre1 = pre_x1 - rate * corr + be1
    pos1 = jnp.maximum(pre1, 0.0)
    act1 = pos1 * pos1
    actb1 = act1.astype(jnp.bfloat16)
    asum1 = jnp.sum(act1, axis=0)
    actb0f = actb0.astype(jnp.float32)
    actb1f = actb1.astype(jnp.float32)
    h10 = jnp.dot(actb1f, actb0f.T, precision=HI)
    rec1_part = rec1_dot(actb1, delta0, wd_flat, lay, width) - c1 * jnp.dot(h10, errb0.astype(jnp.float32), precision=HI)
    rec1 = allreduce(rec1_part, "feat", n_feat)
    errb1 = (rec1 - x1f).astype(jnp.bfloat16)

    e0f = errb0.astype(jnp.float32).reshape(rows, lay, width)
    e1f = errb1.astype(jnp.float32).reshape(rows, lay, width)
    g00 = jnp.einsum("rld,sld->lrs", e0f, e0f, precision=HI)
    g10 = jnp.einsum("rld,sld->lrs", e1f, e0f, precision=HI)
    cross = jnp.einsum("rj,lrj->jl", actb0f, d0, precision=HI)
    quad = jnp.einsum("rj,lrs,sj->jl", actb0f, g00, actb0f, precision=HI)
    sq1 = s0 * s0 * sq0 - 2.0 * c1 * s0 * cross + c1 * c1 * quad
    lens1 = jnp.sqrt(jnp.maximum(sq1, 0.0) + eps)

    d1 = per_layer_dot(errb1, wd_flat, lay, width)
    lowr = jnp.einsum("lrs,sj->lrj", g10, actb0f, precision=HI)
    dd1 = s0.T[:, None, :] * d1 - c1 * lowr
    dact1_part = cst * jnp.sum(dd1, axis=0) + pen * jnp.sum(lens1, axis=1)[None, :]

    g0 = cst - pen * c1 * asum1[:, None] / lens1
    hcoef = pen * (asum0[:, None] / lens0 + asum1[:, None] * s0 / lens1)
    lhs0 = g0.T[:, :, None] * actb0f.T[None, :, :]
    hi0, lo0 = split_bf16(lhs0)
    lhs1 = jnp.broadcast_to((cst * actb1f).T.astype(jnp.bfloat16)[None], (lay, feats, rows))
    lhs = jnp.concatenate([lhs1, hi0, lo0], axis=2)
    lhs_int, h_int = dec_prep(lhs, hcoef)
    rhs = jnp.concatenate([errb1, errb0, errb0], axis=0)
    rhs_st = rhs.reshape(3 * rows, lay, width).transpose(1, 0, 2).reshape(lay * 3 * rows, width)
    x = dact1_part
    dec_step = None
    k = 1
    part = 0
    while k < n_layer:
        x, lhs_int, rhs_st, h_int = lax.optimization_barrier((x, lhs_int, rhs_st, h_int))
        got = lax.ppermute(x, "layer", [(i, i ^ k) for i in range(n_layer)])
        if part < 2:
            dec_step = dec_call(lhs_int, rhs_st, h_int, dec_weight, part, 2, dec_step)
            part += 1
        x = x + got
        x, dec_step = lax.optimization_barrier((x, dec_step))
        k *= 2
    while part < 2:
        dec_step = dec_call(lhs_int, rhs_st, h_int, dec_weight, part, 2, dec_step)
        part += 1
    dact1 = x

    dpre1 = dact1 * 2.0 * pos1
    dpreb1 = dpre1.astype(jnp.bfloat16)
    gbe1 = jnp.sum(dpre1, axis=0)

    dp = jnp.concatenate([dpreb0, dpreb1], axis=0)
    enc = lax.dot_general(xg.reshape(nb * rows, lw), dp, (((0,), (0,)), ((), ())), preferred_element_type=jnp.float32)
    enc_step = enc.astype(jnp.bfloat16).reshape(lay, width, feats)
    bias_step = gbe0 + gbe1
    return (enc_step, dec_step, bias_step)


def solution(mesh):
    n_layer = mesh.shape["layer"]
    n_feat = mesh.shape["feat"]
    in_specs = (
        P(None, "feat", "layer", None),
        P("layer", None, "feat"),
        P("feat", "layer", None),
        P("feat"),
    )
    out_specs = (P("layer", None, "feat"), P("feat", "layer", None), P("feat"))

    def body(a, we, wd, be):
        return per_device(a, we, wd, be, n_layer, n_feat)

    return jax.shard_map(body, mesh=mesh, in_specs=in_specs, out_specs=out_specs, check_vma=False)
```

```python
import jax
import jax.numpy as jnp
from jax import lax
from jax.experimental import pallas as pl
from jax.sharding import PartitionSpec as P

rate = 0.01
penalty = 2.0
eps = 1e-06
HI = lax.Precision.HIGHEST


def normalize(x):
    xf = x.astype(jnp.float32)
    scale = jnp.sqrt(jnp.mean(xf * xf, axis=-1, keepdims=True) + eps)
    return (xf / scale).astype(jnp.bfloat16)


def allreduce(x, axis, n):
    k = 1
    while k < n:
        x = x + lax.ppermute(x, axis, [(i, i ^ k) for i in range(n)])
        k *= 2
    return x


def allgather_rows(x, axis, n):
    me = lax.axis_index(axis)
    k = 1
    while k < n:
        got = lax.ppermute(x, axis, [(i, i ^ k) for i in range(n)])
        low = (me // k) % 2 == 0
        x = jnp.where(low, jnp.concatenate([x, got], axis=1), jnp.concatenate([got, x], axis=1))
        k *= 2
    return x


def split_bf16(v):
    hi = v.astype(jnp.bfloat16)
    lo = (v - hi.astype(jnp.float32)).astype(jnp.bfloat16)
    return hi, lo


def block_rows(e, lay, width):
    rows = e.shape[0]
    e3 = e.reshape(rows, lay, width)
    eye = jnp.eye(lay, dtype=e.dtype)
    blk = eye[:, None, :, None] * e3[None, :, :, :]
    return blk.reshape(lay * rows, lay * width)


def per_layer_dot(e, wd2, lay, width):
    rows = e.shape[0]
    blk = block_rows(e, lay, width)
    out = lax.dot_general(wd2, blk, (((1,), (1,)), ((), ())), preferred_element_type=jnp.float32)
    return out.reshape(wd2.shape[0], lay, rows).transpose(1, 2, 0)


def rec1_dot(actb1, delta, wd2, lay, width):
    rows = actb1.shape[0]
    parts = []
    for l in range(lay):
        cols = slice(l * width, (l + 1) * width)
        corr = (actb1.astype(jnp.float32) * delta[:, l][None, :]).astype(jnp.bfloat16)
        out = jnp.dot(jnp.concatenate([actb1, corr], axis=0), wd2[:, cols], preferred_element_type=jnp.float32)
        parts.append(out[:rows] + out[rows:])
    return jnp.concatenate(parts, axis=1)


def dec_kernel(lhs_ref, rhs_ref, h_ref, wd_ref, out_ref):
    tj, lay, width = wd_ref.shape
    acc = jnp.dot(lhs_ref[...], rhs_ref[...], preferred_element_type=jnp.float32)
    w = wd_ref[...].reshape(tj * lay, width).astype(jnp.float32)
    acc = acc + h_ref[...] * w
    out_ref[...] = acc.astype(out_ref.dtype).reshape(tj, lay, width)


def dec_prep(lhs, hcoef):
    lay, feats, k = lhs.shape
    eye = jnp.eye(lay, dtype=lhs.dtype)
    lhs_int = (eye[None, :, :, None] * lhs.transpose(1, 0, 2)[:, :, None, :]).reshape(feats * lay, lay * k)
    h_int = hcoef.reshape(feats * lay, 1)
    return lhs_int, h_int


def dec_kernel_acc(lhs_ref, rhs_ref, h_ref, wd_ref, prev_ref, out_ref):
    del prev_ref
    dec_kernel(lhs_ref, rhs_ref, h_ref, wd_ref, out_ref)


def dec_call(lhs_int, rhs_st, h_int, wd, part, parts, prev=None):
    feats, lay, width = wd.shape
    k2 = lhs_int.shape[1]
    tj = min(512, feats // parts)
    steps = feats // parts // tj
    off = part * steps
    cost = pl.CostEstimate(
        flops=2 * feats * lay * width * k2 // parts, transcendentals=0, bytes_accessed=4 * feats * lay * width // parts
    )
    in_specs = [
        pl.BlockSpec((tj * lay, k2), lambda j: (j + off, 0)),
        pl.BlockSpec((k2, width), lambda j: (0, 0)),
        pl.BlockSpec((tj * lay, 1), lambda j: (j + off, 0)),
        pl.BlockSpec((tj, lay, width), lambda j: (j + off, 0, 0)),
    ]
    args = [lhs_int, rhs_st, h_int, wd]
    kern, aliases = dec_kernel, {}
    if prev is not None:
        in_specs.append(pl.BlockSpec(memory_space=pl.ANY))
        args.append(prev)
        kern, aliases = dec_kernel_acc, {4: 0}
    return pl.pallas_call(
        kern,
        grid=(steps,),
        in_specs=in_specs,
        out_specs=pl.BlockSpec((tj, lay, width), lambda j: (j + off, 0, 0)),
        out_shape=jax.ShapeDtypeStruct((feats, lay, width), jnp.bfloat16),
        input_output_aliases=aliases,
        cost_estimate=cost,
    )(*args)


def per_device(activations, enc_weight, dec_weight, enc_bias, n_layer, n_feat):
    nb, rloc, lay, width = activations.shape
    feats = enc_weight.shape[2]
    lw = lay * width
    rows = rloc * n_feat
    cst = 2.0 / rows
    pen = penalty / rows
    c1 = rate * cst

    xn = normalize(activations).reshape(nb, rloc, lw)
    xg = allgather_rows(xn, "feat", n_feat)
    x0, x1 = xg[0], xg[1]
    x0f = x0.astype(jnp.float32)
    x1f = x1.astype(jnp.float32)

    we_flat = enc_weight.reshape(lw, feats)
    wd_flat = dec_weight.reshape(feats, lw)

    pre_part = jnp.dot(xg.reshape(nb * rows, lw), we_flat, preferred_element_type=jnp.float32)
    gram = lax.dot_general(x1, x0, (((1,), (1,)), ((), ())), preferred_element_type=jnp.float32)
    gk = -(-(rows * rows) // feats)
    gpad = jnp.pad(gram.reshape(-1), (0, gk * feats - rows * rows)).reshape(gk, feats)
    red1 = allreduce(jnp.concatenate([pre_part[:rows], gpad], axis=0), "layer", n_layer)
    pre_x0 = red1[:rows]
    gram10 = red1[rows:].reshape(-1)[: rows * rows].reshape(rows, rows)
    pre_x1_part = pre_part[rows:]

    sq0 = jnp.stack(
        [jnp.sum(jnp.square(wd_flat[:, l * width : (l + 1) * width].astype(jnp.float32)), axis=1) for l in range(lay)],
        axis=1,
    )
    lens0 = jnp.sqrt(sq0 + eps)

    pre0 = pre_x0 + enc_bias
    pos0 = jnp.maximum(pre0, 0.0)
    act0 = pos0 * pos0
    actb0 = act0.astype(jnp.bfloat16)
    asum0 = jnp.sum(act0, axis=0)
    rec0 = allreduce(jnp.dot(actb0, wd_flat, preferred_element_type=jnp.float32), "feat", n_feat)
    errb0 = (rec0 - x0f).astype(jnp.bfloat16)
    d0 = per_layer_dot(errb0, wd_flat, lay, width)
    dact0_part = cst * jnp.sum(d0, axis=0) + pen * jnp.sum(lens0, axis=1)[None, :]
    red3 = allreduce(jnp.concatenate([dact0_part, pre_x1_part], axis=0), "layer", n_layer)
    dact0 = red3[:rows]
    pre_x1 = red3[rows:]
    dpre0 = dact0 * 2.0 * pos0
    dpreb0 = dpre0.astype(jnp.bfloat16)
    gbe0 = jnp.sum(dpre0, axis=0)

    delta0 = -rate * pen * asum0[:, None] / lens0
    s0 = 1.0 + delta0
    be1 = enc_bias - rate * gbe0
    corr = jnp.dot(gram10, dpreb0.astype(jnp.float32), precision=HI)
    pre1 = pre_x1 - rate * corr + be1
    pos1 = jnp.maximum(pre1, 0.0)
    act1 = pos1 * pos1
    actb1 = act1.astype(jnp.bfloat16)
    asum1 = jnp.sum(act1, axis=0)
    actb0f = actb0.astype(jnp.float32)
    actb1f = actb1.astype(jnp.float32)
    h10 = jnp.dot(actb1f, actb0f.T, precision=HI)
    rec1_part = rec1_dot(actb1, delta0, wd_flat, lay, width) - c1 * jnp.dot(h10, errb0.astype(jnp.float32), precision=HI)
    rec1 = allreduce(rec1_part, "feat", n_feat)
    errb1 = (rec1 - x1f).astype(jnp.bfloat16)

    e0f = errb0.astype(jnp.float32).reshape(rows, lay, width)
    e1f = errb1.astype(jnp.float32).reshape(rows, lay, width)
    g00 = jnp.einsum("rld,sld->lrs", e0f, e0f, precision=HI)
    g10 = jnp.einsum("rld,sld->lrs", e1f, e0f, precision=HI)
    cross = jnp.einsum("rj,lrj->jl", actb0f, d0, precision=HI)
    quad = jnp.einsum("rj,lrs,sj->jl", actb0f, g00, actb0f, precision=HI)
    sq1 = s0 * s0 * sq0 - 2.0 * c1 * s0 * cross + c1 * c1 * quad
    lens1 = jnp.sqrt(jnp.maximum(sq1, 0.0) + eps)

    d1 = per_layer_dot(errb1, wd_flat, lay, width)
    lowr = jnp.einsum("lrs,sj->lrj", g10, actb0f, precision=HI)
    dd1 = s0.T[:, None, :] * d1 - c1 * lowr
    dact1_part = cst * jnp.sum(dd1, axis=0) + pen * jnp.sum(lens1, axis=1)[None, :]

    g0 = cst - pen * c1 * asum1[:, None] / lens1
    hcoef = pen * (asum0[:, None] / lens0 + asum1[:, None] * s0 / lens1)
    lhs0 = g0.T[:, :, None] * actb0f.T[None, :, :]
    hi0, lo0 = split_bf16(lhs0)
    lhs1 = jnp.broadcast_to((cst * actb1f).T.astype(jnp.bfloat16)[None], (lay, feats, rows))
    lhs = jnp.concatenate([lhs1, hi0, lo0], axis=2)
    lhs_int, h_int = dec_prep(lhs, hcoef)
    rhs = jnp.concatenate([errb1, errb0, errb0], axis=0)
    rhs_st = rhs.reshape(3 * rows, lay, width).transpose(1, 0, 2).reshape(lay * 3 * rows, width)
    x = dact1_part
    dec_step = None
    k = 1
    part = 0
    while k < n_layer:
        x, lhs_int, rhs_st, h_int = lax.optimization_barrier((x, lhs_int, rhs_st, h_int))
        got = lax.ppermute(x, "layer", [(i, i ^ k) for i in range(n_layer)])
        if part < 2:
            dec_step = dec_call(lhs_int, rhs_st, h_int, dec_weight, part, 2, dec_step)
            part += 1
        x = x + got
        x, dec_step = lax.optimization_barrier((x, dec_step))
        k *= 2
    while part < 2:
        dec_step = dec_call(lhs_int, rhs_st, h_int, dec_weight, part, 2, dec_step)
        part += 1
    dact1 = x

    dpre1 = dact1 * 2.0 * pos1
    dpreb1 = dpre1.astype(jnp.bfloat16)
    gbe1 = jnp.sum(dpre1, axis=0)

    dp = jnp.concatenate([dpreb0, dpreb1], axis=0)
    enc = lax.dot_general(xg.reshape(nb * rows, lw), dp, (((0,), (0,)), ((), ())), preferred_element_type=jnp.float32)
    enc_step = enc.astype(jnp.bfloat16).reshape(lay, width, feats)
    bias_step = gbe0 + gbe1
    return (enc_step, dec_step, bias_step)


def solution(mesh):
    n_layer = mesh.shape["layer"]
    n_feat = mesh.shape["feat"]
    in_specs = (
        P(None, "feat", "layer", None),
        P("layer", None, "feat"),
        P("feat", "layer", None),
        P("feat"),
    )
    out_specs = (P("layer", None, "feat"), P("feat", "layer", None), P("feat"))

    def body(a, we, wd, be):
        return per_device(a, we, wd, be, n_layer, n_feat)

    return jax.shard_map(body, mesh=mesh, in_specs=in_specs, out_specs=out_specs, check_vma=False)
```

```python
import jax
import jax.numpy as jnp
from jax import lax
from jax.experimental import pallas as pl
from jax.sharding import PartitionSpec as P

rate = 0.01
penalty = 2.0
eps = 1e-06
HI = lax.Precision.HIGHEST


def normalize(x):
    xf = x.astype(jnp.float32)
    scale = jnp.sqrt(jnp.mean(xf * xf, axis=-1, keepdims=True) + eps)
    return (xf / scale).astype(jnp.bfloat16)


def allreduce(x, axis, n):
    k = 1
    while k < n:
        x = x + lax.ppermute(x, axis, [(i, i ^ k) for i in range(n)])
        k *= 2
    return x


def allgather_rows(x, axis, n):
    me = lax.axis_index(axis)
    k = 1
    while k < n:
        got = lax.ppermute(x, axis, [(i, i ^ k) for i in range(n)])
        low = (me // k) % 2 == 0
        x = jnp.where(low, jnp.concatenate([x, got], axis=1), jnp.concatenate([got, x], axis=1))
        k *= 2
    return x


def split_bf16(v):
    hi = v.astype(jnp.bfloat16)
    lo = (v - hi.astype(jnp.float32)).astype(jnp.bfloat16)
    return hi, lo


def block_rows(e, lay, width):
    rows = e.shape[0]
    e3 = e.reshape(rows, lay, width)
    eye = jnp.eye(lay, dtype=e.dtype)
    blk = eye[:, None, :, None] * e3[None, :, :, :]
    return blk.reshape(lay * rows, lay * width)


def per_layer_dot(e, wd2, lay, width):
    outs = []
    for l in range(lay):
        cols = slice(l * width, (l + 1) * width)
        outs.append(lax.dot_general(wd2[:, cols], e[:, cols], (((1,), (1,)), ((), ())), preferred_element_type=jnp.float32))
    return jnp.stack(outs, axis=0).transpose(0, 2, 1)


def rec1_dot(actb1, delta, wd2, lay, width):
    rows = actb1.shape[0]
    parts = []
    for l in range(lay):
        cols = slice(l * width, (l + 1) * width)
        corr = (actb1.astype(jnp.float32) * delta[:, l][None, :]).astype(jnp.bfloat16)
        out = jnp.dot(jnp.concatenate([actb1, corr], axis=0), wd2[:, cols], preferred_element_type=jnp.float32)
        parts.append(out[:rows] + out[rows:])
    return jnp.concatenate(parts, axis=1)


def dec_kernel(lhs_ref, rhs_ref, h_ref, wd_ref, out_ref):
    tj, lay, width = wd_ref.shape
    acc = jnp.dot(lhs_ref[...], rhs_ref[...], preferred_element_type=jnp.float32)
    w = wd_ref[...].reshape(tj * lay, width).astype(jnp.float32)
    acc = acc + h_ref[:, 0:1] * w
    out_ref[...] = acc.astype(out_ref.dtype).reshape(tj, lay, width)


def dec_prep(lhs, hcoef):
    lay, feats, k = lhs.shape
    eye = jnp.eye(lay, dtype=lhs.dtype)
    lhs_int = (eye[None, :, :, None] * lhs.transpose(1, 0, 2)[:, :, None, :]).reshape(feats * lay, lay * k)
    h_int = jnp.broadcast_to(hcoef.reshape(feats * lay, 1), (feats * lay, 128))
    return lhs_int, h_int


def dec_kernel_acc(lhs_ref, rhs_ref, h_ref, wd_ref, prev_ref, out_ref):
    del prev_ref
    dec_kernel(lhs_ref, rhs_ref, h_ref, wd_ref, out_ref)


def dec_call(lhs_int, rhs_st, h_int, wd, part, parts, prev=None):
    feats, lay, width = wd.shape
    k2 = lhs_int.shape[1]
    tj = min(256, feats // parts)
    steps = feats // parts // tj
    off = part * steps
    cost = pl.CostEstimate(
        flops=2 * feats * lay * width * k2 // parts, transcendentals=0, bytes_accessed=4 * feats * lay * width // parts
    )
    in_specs = [
        pl.BlockSpec((tj * lay, k2), lambda j: (j + off, 0)),
        pl.BlockSpec((k2, width), lambda j: (0, 0)),
        pl.BlockSpec((tj * lay, 128), lambda j: (j + off, 0)),
        pl.BlockSpec((tj, lay, width), lambda j: (j + off, 0, 0)),
    ]
    args = [lhs_int, rhs_st, h_int, wd]
    kern, aliases = dec_kernel, {}
    if prev is not None:
        in_specs.append(pl.BlockSpec(memory_space=pl.ANY))
        args.append(prev)
        kern, aliases = dec_kernel_acc, {4: 0}
    return pl.pallas_call(
        kern,
        grid=(steps,),
        in_specs=in_specs,
        out_specs=pl.BlockSpec((tj, lay, width), lambda j: (j + off, 0, 0)),
        out_shape=jax.ShapeDtypeStruct((feats, lay, width), jnp.bfloat16),
        input_output_aliases=aliases,
        cost_estimate=cost,
    )(*args)


def per_device(activations, enc_weight, dec_weight, enc_bias, n_layer, n_feat):
    nb, rloc, lay, width = activations.shape
    feats = enc_weight.shape[2]
    lw = lay * width
    rows = rloc * n_feat
    cst = 2.0 / rows
    pen = penalty / rows
    c1 = rate * cst

    xn = normalize(activations).reshape(nb, rloc, lw)
    xg = allgather_rows(xn, "feat", n_feat)
    x0, x1 = xg[0], xg[1]
    x0f = x0.astype(jnp.float32)
    x1f = x1.astype(jnp.float32)

    we_flat = enc_weight.reshape(lw, feats)
    wd_flat = dec_weight.reshape(feats, lw)

    pre_part = jnp.dot(xg.reshape(nb * rows, lw), we_flat, preferred_element_type=jnp.float32)
    gram = lax.dot_general(x1, x0, (((1,), (1,)), ((), ())), preferred_element_type=jnp.float32)
    gk = -(-(rows * rows) // feats)
    gpad = jnp.pad(gram.reshape(-1), (0, gk * feats - rows * rows)).reshape(gk, feats)
    red1 = allreduce(jnp.concatenate([pre_part[:rows], gpad], axis=0), "layer", n_layer)
    pre_x0 = red1[:rows]
    gram10 = red1[rows:].reshape(-1)[: rows * rows].reshape(rows, rows)
    pre_x1_part = pre_part[rows:]

    sq0 = jnp.stack(
        [jnp.sum(jnp.square(wd_flat[:, l * width : (l + 1) * width].astype(jnp.float32)), axis=1) for l in range(lay)],
        axis=1,
    )
    lens0 = jnp.sqrt(sq0 + eps)

    pre0 = pre_x0 + enc_bias
    pos0 = jnp.maximum(pre0, 0.0)
    act0 = pos0 * pos0
    actb0 = act0.astype(jnp.bfloat16)
    asum0 = jnp.sum(act0, axis=0)
    rec0 = allreduce(jnp.dot(actb0, wd_flat, preferred_element_type=jnp.float32), "feat", n_feat)
    errb0 = (rec0 - x0f).astype(jnp.bfloat16)
    d0 = per_layer_dot(errb0, wd_flat, lay, width)
    dact0_part = cst * jnp.sum(d0, axis=0) + pen * jnp.sum(lens0, axis=1)[None, :]
    red3 = allreduce(jnp.concatenate([dact0_part, pre_x1_part], axis=0), "layer", n_layer)
    dact0 = red3[:rows]
    pre_x1 = red3[rows:]
    dpre0 = dact0 * 2.0 * pos0
    dpreb0 = dpre0.astype(jnp.bfloat16)
    gbe0 = jnp.sum(dpre0, axis=0)

    delta0 = -rate * pen * asum0[:, None] / lens0
    s0 = 1.0 + delta0
    be1 = enc_bias - rate * gbe0
    corr = jnp.dot(gram10, dpreb0.astype(jnp.float32), precision=HI)
    pre1 = pre_x1 - rate * corr + be1
    pos1 = jnp.maximum(pre1, 0.0)
    act1 = pos1 * pos1
    actb1 = act1.astype(jnp.bfloat16)
    asum1 = jnp.sum(act1, axis=0)
    actb0f = actb0.astype(jnp.float32)
    actb1f = actb1.astype(jnp.float32)
    h10 = jnp.dot(actb1f, actb0f.T, precision=HI)
    rec1_part = rec1_dot(actb1, delta0, wd_flat, lay, width) - c1 * jnp.dot(h10, errb0.astype(jnp.float32), precision=HI)
    rec1 = allreduce(rec1_part, "feat", n_feat)
    errb1 = (rec1 - x1f).astype(jnp.bfloat16)

    e0f = errb0.astype(jnp.float32).reshape(rows, lay, width)
    e1f = errb1.astype(jnp.float32).reshape(rows, lay, width)
    g00 = jnp.einsum("rld,sld->lrs", e0f, e0f, precision=HI)
    g10 = jnp.einsum("rld,sld->lrs", e1f, e0f, precision=HI)
    cross = jnp.einsum("rj,lrj->jl", actb0f, d0, precision=HI)
    quad = jnp.einsum("rj,lrs,sj->jl", actb0f, g00, actb0f, precision=HI)
    sq1 = s0 * s0 * sq0 - 2.0 * c1 * s0 * cross + c1 * c1 * quad
    lens1 = jnp.sqrt(jnp.maximum(sq1, 0.0) + eps)

    d1 = per_layer_dot(errb1, wd_flat, lay, width)
    lowr = jnp.einsum("lrs,sj->lrj", g10, actb0f, precision=HI)
    dd1 = s0.T[:, None, :] * d1 - c1 * lowr
    dact1_part = cst * jnp.sum(dd1, axis=0) + pen * jnp.sum(lens1, axis=1)[None, :]

    g0 = cst - pen * c1 * asum1[:, None] / lens1
    hcoef = pen * (asum0[:, None] / lens0 + asum1[:, None] * s0 / lens1)
    lhs0 = g0.T[:, :, None] * actb0f.T[None, :, :]
    hi0, lo0 = split_bf16(lhs0)
    lhs1 = jnp.broadcast_to((cst * actb1f).T.astype(jnp.bfloat16)[None], (lay, feats, rows))
    lhs = jnp.concatenate([lhs1, hi0, lo0], axis=2)
    lhs_int, h_int = dec_prep(lhs, hcoef)
    rhs = jnp.concatenate([errb1, errb0, errb0], axis=0)
    rhs_st = rhs.reshape(3 * rows, lay, width).transpose(1, 0, 2).reshape(lay * 3 * rows, width)
    x = dact1_part
    dec_step = None
    k = 1
    part = 0
    while k < n_layer:
        x, lhs_int, rhs_st, h_int = lax.optimization_barrier((x, lhs_int, rhs_st, h_int))
        got = lax.ppermute(x, "layer", [(i, i ^ k) for i in range(n_layer)])
        if part < 2:
            dec_step = dec_call(lhs_int, rhs_st, h_int, dec_weight, part, 2, dec_step)
            part += 1
        x = x + got
        x, dec_step = lax.optimization_barrier((x, dec_step))
        k *= 2
    while part < 2:
        dec_step = dec_call(lhs_int, rhs_st, h_int, dec_weight, part, 2, dec_step)
        part += 1
    dact1 = x

    dpre1 = dact1 * 2.0 * pos1
    dpreb1 = dpre1.astype(jnp.bfloat16)
    gbe1 = jnp.sum(dpre1, axis=0)

    dp = jnp.concatenate([dpreb0, dpreb1], axis=0)
    enc = lax.dot_general(xg.reshape(nb * rows, lw), dp, (((0,), (0,)), ((), ())), preferred_element_type=jnp.float32)
    enc_step = enc.astype(jnp.bfloat16).reshape(lay, width, feats)
    bias_step = gbe0 + gbe1
    return (enc_step, dec_step, bias_step)


def solution(mesh):
    n_layer = mesh.shape["layer"]
    n_feat = mesh.shape["feat"]
    in_specs = (
        P(None, "feat", "layer", None),
        P("layer", None, "feat"),
        P("feat", "layer", None),
        P("feat"),
    )
    out_specs = (P("layer", None, "feat"), P("feat", "layer", None), P("feat"))

    def body(a, we, wd, be):
        return per_device(a, we, wd, be, n_layer, n_feat)

    return jax.shard_map(body, mesh=mesh, in_specs=in_specs, out_specs=out_specs, check_vma=False)
```

```python
import jax
import jax.numpy as jnp
from jax import lax
from jax.experimental import pallas as pl
from jax.sharding import PartitionSpec as P

rate = 0.01
penalty = 2.0
eps = 1e-06
HI = lax.Precision.HIGHEST


def normalize(x):
    xf = x.astype(jnp.float32)
    scale = jnp.sqrt(jnp.mean(xf * xf, axis=-1, keepdims=True) + eps)
    return (xf / scale).astype(jnp.bfloat16)


def allreduce(x, axis, n):
    k = 1
    while k < n:
        x = x + lax.ppermute(x, axis, [(i, i ^ k) for i in range(n)])
        k *= 2
    return x


def allgather_rows(x, axis, n):
    me = lax.axis_index(axis)
    k = 1
    while k < n:
        got = lax.ppermute(x, axis, [(i, i ^ k) for i in range(n)])
        low = (me // k) % 2 == 0
        x = jnp.where(low, jnp.concatenate([x, got], axis=1), jnp.concatenate([got, x], axis=1))
        k *= 2
    return x


def split_bf16(v):
    hi = v.astype(jnp.bfloat16)
    lo = (v - hi.astype(jnp.float32)).astype(jnp.bfloat16)
    return hi, lo


def block_rows(e, lay, width):
    rows = e.shape[0]
    e3 = e.reshape(rows, lay, width)
    eye = jnp.eye(lay, dtype=e.dtype)
    blk = eye[:, None, :, None] * e3[None, :, :, :]
    return blk.reshape(lay * rows, lay * width)


def per_layer_dot(e, wd2, lay, width):
    outs = []
    for l in range(lay):
        cols = slice(l * width, (l + 1) * width)
        outs.append(lax.dot_general(wd2[:, cols], e[:, cols], (((1,), (1,)), ((), ())), preferred_element_type=jnp.float32))
    return jnp.stack(outs, axis=0).transpose(0, 2, 1)


def rec1_dot(actb1, delta, wd2, lay, width):
    rows = actb1.shape[0]
    parts = []
    for l in range(lay):
        cols = slice(l * width, (l + 1) * width)
        corr = (actb1.astype(jnp.float32) * delta[:, l][None, :]).astype(jnp.bfloat16)
        out = jnp.dot(jnp.concatenate([actb1, corr], axis=0), wd2[:, cols], preferred_element_type=jnp.float32)
        parts.append(out[:rows] + out[rows:])
    return jnp.concatenate(parts, axis=1)


def dec_kernel(lhs_ref, rhs_ref, h_ref, wd_ref, out_ref):
    tj, lay, width = wd_ref.shape
    acc = jnp.dot(lhs_ref[...], rhs_ref[...], preferred_element_type=jnp.float32)
    w = wd_ref[...].reshape(tj * lay, width).astype(jnp.float32)
    acc = acc + h_ref[:, 0:1] * w
    out_ref[...] = acc.astype(out_ref.dtype).reshape(tj, lay, width)


def dec_prep(lhs, hcoef):
    lay, feats, k = lhs.shape
    eye = jnp.eye(lay, dtype=lhs.dtype)
    lhs_int = (eye[None, :, :, None] * lhs.transpose(1, 0, 2)[:, :, None, :]).reshape(feats * lay, lay * k)
    h_int = jnp.broadcast_to(hcoef.reshape(feats * lay, 1), (feats * lay, 128))
    return lhs_int, h_int


def dec_kernel_acc(lhs_ref, rhs_ref, h_ref, wd_ref, prev_ref, out_ref):
    del prev_ref
    dec_kernel(lhs_ref, rhs_ref, h_ref, wd_ref, out_ref)


def dec_call(lhs_int, rhs_st, h_int, wd, part, parts, prev=None):
    feats, lay, width = wd.shape
    k2 = lhs_int.shape[1]
    tj = min(256, feats // parts)
    steps = feats // parts // tj
    off = part * steps
    cost = pl.CostEstimate(
        flops=2 * feats * lay * width * k2 // parts, transcendentals=0, bytes_accessed=4 * feats * lay * width // parts
    )
    in_specs = [
        pl.BlockSpec((tj * lay, k2), lambda j: (j + off, 0)),
        pl.BlockSpec((k2, width), lambda j: (0, 0)),
        pl.BlockSpec((tj * lay, 128), lambda j: (j + off, 0)),
        pl.BlockSpec((tj, lay, width), lambda j: (j + off, 0, 0)),
    ]
    args = [lhs_int, rhs_st, h_int, wd]
    kern, aliases = dec_kernel, {}
    if prev is not None:
        in_specs.append(pl.BlockSpec(memory_space=pl.ANY))
        args.append(prev)
        kern, aliases = dec_kernel_acc, {4: 0}
    return pl.pallas_call(
        kern,
        grid=(steps,),
        in_specs=in_specs,
        out_specs=pl.BlockSpec((tj, lay, width), lambda j: (j + off, 0, 0)),
        out_shape=jax.ShapeDtypeStruct((feats, lay, width), jnp.bfloat16),
        input_output_aliases=aliases,
        cost_estimate=cost,
    )(*args)


def per_device(activations, enc_weight, dec_weight, enc_bias, n_layer, n_feat):
    nb, rloc, lay, width = activations.shape
    feats = enc_weight.shape[2]
    lw = lay * width
    rows = rloc * n_feat
    cst = 2.0 / rows
    pen = penalty / rows
    c1 = rate * cst

    xn = normalize(activations).reshape(nb, rloc, lw)
    xg = allgather_rows(xn, "feat", n_feat)
    x0, x1 = xg[0], xg[1]
    x0f = x0.astype(jnp.float32)
    x1f = x1.astype(jnp.float32)

    we_flat = enc_weight.reshape(lw, feats)
    wd_flat = dec_weight.reshape(feats, lw)

    pre_part = jnp.dot(xg.reshape(nb * rows, lw), we_flat, preferred_element_type=jnp.float32)
    gram = lax.dot_general(x1, x0, (((1,), (1,)), ((), ())), preferred_element_type=jnp.float32)
    gk = -(-(rows * rows) // feats)
    gpad = jnp.pad(gram.reshape(-1), (0, gk * feats - rows * rows)).reshape(gk, feats)
    red1 = allreduce(jnp.concatenate([pre_part, gpad], axis=0), "layer", n_layer)
    pre_x0 = red1[:rows]
    pre_x1 = red1[rows : 2 * rows]
    gram10 = red1[2 * rows :].reshape(-1)[: rows * rows].reshape(rows, rows)

    sq0 = jnp.stack(
        [jnp.sum(jnp.square(wd_flat[:, l * width : (l + 1) * width].astype(jnp.float32)), axis=1) for l in range(lay)],
        axis=1,
    )
    lens0 = jnp.sqrt(sq0 + eps)

    pre0 = pre_x0 + enc_bias
    pos0 = jnp.maximum(pre0, 0.0)
    act0 = pos0 * pos0
    actb0 = act0.astype(jnp.bfloat16)
    asum0 = jnp.sum(act0, axis=0)
    rec0 = allreduce(jnp.dot(actb0, wd_flat, preferred_element_type=jnp.float32), "feat", n_feat)
    errb0 = (rec0 - x0f).astype(jnp.bfloat16)
    d0 = per_layer_dot(errb0, wd_flat, lay, width)
    dact0_part = cst * jnp.sum(d0, axis=0) + pen * jnp.sum(lens0, axis=1)[None, :]
    dact0 = allreduce(dact0_part, "layer", n_layer)
    dpre0 = dact0 * 2.0 * pos0
    dpreb0 = dpre0.astype(jnp.bfloat16)
    gbe0 = jnp.sum(dpre0, axis=0)

    delta0 = -rate * pen * asum0[:, None] / lens0
    s0 = 1.0 + delta0
    be1 = enc_bias - rate * gbe0
    corr = jnp.dot(gram10, dpreb0.astype(jnp.float32), precision=HI)
    pre1 = pre_x1 - rate * corr + be1
    pos1 = jnp.maximum(pre1, 0.0)
    act1 = pos1 * pos1
    actb1 = act1.astype(jnp.bfloat16)
    asum1 = jnp.sum(act1, axis=0)
    actb0f = actb0.astype(jnp.float32)
    actb1f = actb1.astype(jnp.float32)
    h10 = jnp.dot(actb1f, actb0f.T, precision=HI)
    rec1_part = rec1_dot(actb1, delta0, wd_flat, lay, width) - c1 * jnp.dot(h10, errb0.astype(jnp.float32), precision=HI)
    rec1 = allreduce(rec1_part, "feat", n_feat)
    errb1 = (rec1 - x1f).astype(jnp.bfloat16)

    e0f = errb0.astype(jnp.float32).reshape(rows, lay, width)
    e1f = errb1.astype(jnp.float32).reshape(rows, lay, width)
    g00 = jnp.einsum("rld,sld->lrs", e0f, e0f, precision=HI)
    g10 = jnp.einsum("rld,sld->lrs", e1f, e0f, precision=HI)
    cross = jnp.einsum("rj,lrj->jl", actb0f, d0, precision=HI)
    quad = jnp.einsum("rj,lrs,sj->jl", actb0f, g00, actb0f, precision=HI)
    sq1 = s0 * s0 * sq0 - 2.0 * c1 * s0 * cross + c1 * c1 * quad
    lens1 = jnp.sqrt(jnp.maximum(sq1, 0.0) + eps)

    d1 = per_layer_dot(errb1, wd_flat, lay, width)
    lowr = jnp.einsum("lrs,sj->lrj", g10, actb0f, precision=HI)
    dd1 = s0.T[:, None, :] * d1 - c1 * lowr
    dact1_part = cst * jnp.sum(dd1, axis=0) + pen * jnp.sum(lens1, axis=1)[None, :]

    g0 = cst - pen * c1 * asum1[:, None] / lens1
    hcoef = pen * (asum0[:, None] / lens0 + asum1[:, None] * s0 / lens1)
    lhs0 = g0.T[:, :, None] * actb0f.T[None, :, :]
    hi0, lo0 = split_bf16(lhs0)
    lhs1 = jnp.broadcast_to((cst * actb1f).T.astype(jnp.bfloat16)[None], (lay, feats, rows))
    lhs = jnp.concatenate([lhs1, hi0, lo0], axis=2)
    lhs_int, h_int = dec_prep(lhs, hcoef)
    rhs = jnp.concatenate([errb1, errb0, errb0], axis=0)
    rhs_st = rhs.reshape(3 * rows, lay, width).transpose(1, 0, 2).reshape(lay * 3 * rows, width)
    x = dact1_part
    dec_step = None
    k = 1
    part = 0
    while k < n_layer:
        x, lhs_int, rhs_st, h_int = lax.optimization_barrier((x, lhs_int, rhs_st, h_int))
        got = lax.ppermute(x, "layer", [(i, i ^ k) for i in range(n_layer)])
        if part < 2:
            dec_step = dec_call(lhs_int, rhs_st, h_int, dec_weight, part, 2, dec_step)
            part += 1
        x = x + got
        x, dec_step = lax.optimization_barrier((x, dec_step))
        k *= 2
    while part < 2:
        dec_step = dec_call(lhs_int, rhs_st, h_int, dec_weight, part, 2, dec_step)
        part += 1
    dact1 = x

    dpre1 = dact1 * 2.0 * pos1
    dpreb1 = dpre1.astype(jnp.bfloat16)
    gbe1 = jnp.sum(dpre1, axis=0)

    dp = jnp.concatenate([dpreb0, dpreb1], axis=0)
    enc = lax.dot_general(xg.reshape(nb * rows, lw), dp, (((0,), (0,)), ((), ())), preferred_element_type=jnp.float32)
    enc_step = enc.astype(jnp.bfloat16).reshape(lay, width, feats)
    bias_step = gbe0 + gbe1
    return (enc_step, dec_step, bias_step)


def solution(mesh):
    n_layer = mesh.shape["layer"]
    n_feat = mesh.shape["feat"]
    in_specs = (
        P(None, "feat", "layer", None),
        P("layer", None, "feat"),
        P("feat", "layer", None),
        P("feat"),
    )
    out_specs = (P("layer", None, "feat"), P("feat", "layer", None), P("feat"))

    def body(a, we, wd, be):
        return per_device(a, we, wd, be, n_layer, n_feat)

    return jax.shard_map(body, mesh=mesh, in_specs=in_specs, out_specs=out_specs, check_vma=False)
```

```python
import jax
import jax.numpy as jnp
from jax import lax
from jax.experimental import pallas as pl
from jax.sharding import PartitionSpec as P

rate = 0.01
penalty = 2.0
eps = 1e-06
HI = lax.Precision.HIGHEST


def normalize(x):
    xf = x.astype(jnp.float32)
    scale = jnp.sqrt(jnp.mean(xf * xf, axis=-1, keepdims=True) + eps)
    return (xf / scale).astype(jnp.bfloat16)


def allreduce(x, axis, n):
    k = 1
    while k < n:
        x = x + lax.ppermute(x, axis, [(i, i ^ k) for i in range(n)])
        k *= 2
    return x


def allgather_rows(x, axis, n):
    me = lax.axis_index(axis)
    k = 1
    while k < n:
        got = lax.ppermute(x, axis, [(i, i ^ k) for i in range(n)])
        low = (me // k) % 2 == 0
        x = jnp.where(low, jnp.concatenate([x, got], axis=1), jnp.concatenate([got, x], axis=1))
        k *= 2
    return x


def split_bf16(v):
    hi = v.astype(jnp.bfloat16)
    lo = (v - hi.astype(jnp.float32)).astype(jnp.bfloat16)
    return hi, lo


def block_rows(e, lay, width):
    rows = e.shape[0]
    e3 = e.reshape(rows, lay, width)
    eye = jnp.eye(lay, dtype=e.dtype)
    blk = eye[:, None, :, None] * e3[None, :, :, :]
    return blk.reshape(lay * rows, lay * width)


def per_layer_dot(e, wd2, lay, width):
    outs = []
    for l in range(lay):
        cols = slice(l * width, (l + 1) * width)
        outs.append(lax.dot_general(wd2[:, cols], e[:, cols], (((1,), (1,)), ((), ())), preferred_element_type=jnp.float32))
    return jnp.stack(outs, axis=0).transpose(0, 2, 1)


def rec1_dot(actb1, delta, wd2, lay, width):
    rows = actb1.shape[0]
    parts = []
    for l in range(lay):
        cols = slice(l * width, (l + 1) * width)
        corr = (actb1.astype(jnp.float32) * delta[:, l][None, :]).astype(jnp.bfloat16)
        out = jnp.dot(jnp.concatenate([actb1, corr], axis=0), wd2[:, cols], preferred_element_type=jnp.float32)
        parts.append(out[:rows] + out[rows:])
    return jnp.concatenate(parts, axis=1)


def dec_kernel(lhs_ref, rhs_ref, h_ref, wd_ref, out_ref):
    tj, lay, width = wd_ref.shape
    acc = jnp.dot(lhs_ref[...], rhs_ref[...], preferred_element_type=jnp.float32)
    w = wd_ref[...].reshape(tj * lay, width).astype(jnp.float32)
    acc = acc + h_ref[:, 0:1] * w
    out_ref[...] = acc.astype(out_ref.dtype).reshape(tj, lay, width)


def dec_prep(lhs, hcoef):
    lay, feats, k = lhs.shape
    eye = jnp.eye(lay, dtype=lhs.dtype)
    lhs_int = (eye[None, :, :, None] * lhs.transpose(1, 0, 2)[:, :, None, :]).reshape(feats * lay, lay * k)
    h_int = jnp.broadcast_to(hcoef.reshape(feats * lay, 1), (feats * lay, 128))
    return lhs_int, h_int


def dec_kernel_acc(lhs_ref, rhs_ref, h_ref, wd_ref, prev_ref, out_ref):
    del prev_ref
    dec_kernel(lhs_ref, rhs_ref, h_ref, wd_ref, out_ref)


def dec_call(lhs_int, rhs_st, h_int, wd, part, parts, prev=None):
    feats, lay, width = wd.shape
    k2 = lhs_int.shape[1]
    tj = min(512, feats // parts)
    steps = feats // parts // tj
    off = part * steps
    cost = pl.CostEstimate(
        flops=2 * feats * lay * width * k2 // parts, transcendentals=0, bytes_accessed=4 * feats * lay * width // parts
    )
    in_specs = [
        pl.BlockSpec((tj * lay, k2), lambda j: (j + off, 0)),
        pl.BlockSpec((k2, width), lambda j: (0, 0)),
        pl.BlockSpec((tj * lay, 128), lambda j: (j + off, 0)),
        pl.BlockSpec((tj, lay, width), lambda j: (j + off, 0, 0)),
    ]
    args = [lhs_int, rhs_st, h_int, wd]
    kern, aliases = dec_kernel, {}
    if prev is not None:
        in_specs.append(pl.BlockSpec(memory_space=pl.ANY))
        args.append(prev)
        kern, aliases = dec_kernel_acc, {4: 0}
    return pl.pallas_call(
        kern,
        grid=(steps,),
        in_specs=in_specs,
        out_specs=pl.BlockSpec((tj, lay, width), lambda j: (j + off, 0, 0)),
        out_shape=jax.ShapeDtypeStruct((feats, lay, width), jnp.bfloat16),
        input_output_aliases=aliases,
        cost_estimate=cost,
    )(*args)


def per_device(activations, enc_weight, dec_weight, enc_bias, n_layer, n_feat):
    nb, rloc, lay, width = activations.shape
    feats = enc_weight.shape[2]
    lw = lay * width
    rows = rloc * n_feat
    cst = 2.0 / rows
    pen = penalty / rows
    c1 = rate * cst

    xn = normalize(activations).reshape(nb, rloc, lw)
    xg = allgather_rows(xn, "feat", n_feat)
    x0, x1 = xg[0], xg[1]
    x0f = x0.astype(jnp.float32)
    x1f = x1.astype(jnp.float32)

    we_flat = enc_weight.reshape(lw, feats)
    wd_flat = dec_weight.reshape(feats, lw)

    pre_part = jnp.dot(xg.reshape(nb * rows, lw), we_flat, preferred_element_type=jnp.float32)
    gram = lax.dot_general(x1, x0, (((1,), (1,)), ((), ())), preferred_element_type=jnp.float32)
    gk = -(-(rows * rows) // feats)
    gpad = jnp.pad(gram.reshape(-1), (0, gk * feats - rows * rows)).reshape(gk, feats)
    red1 = allreduce(jnp.concatenate([pre_part[:rows], gpad], axis=0), "layer", n_layer)
    pre_x0 = red1[:rows]
    gram10 = red1[rows:].reshape(-1)[: rows * rows].reshape(rows, rows)
    pre_x1_part = pre_part[rows:]

    sq0 = jnp.stack(
        [jnp.sum(jnp.square(wd_flat[:, l * width : (l + 1) * width].astype(jnp.float32)), axis=1) for l in range(lay)],
        axis=1,
    )
    lens0 = jnp.sqrt(sq0 + eps)

    pre0 = pre_x0 + enc_bias
    pos0 = jnp.maximum(pre0, 0.0)
    act0 = pos0 * pos0
    actb0 = act0.astype(jnp.bfloat16)
    asum0 = jnp.sum(act0, axis=0)
    rec0 = allreduce(jnp.dot(actb0, wd_flat, preferred_element_type=jnp.float32), "feat", n_feat)
    errb0 = (rec0 - x0f).astype(jnp.bfloat16)
    d0 = per_layer_dot(errb0, wd_flat, lay, width)
    dact0_part = cst * jnp.sum(d0, axis=0) + pen * jnp.sum(lens0, axis=1)[None, :]
    red3 = allreduce(jnp.concatenate([dact0_part, pre_x1_part], axis=0), "layer", n_layer)
    dact0 = red3[:rows]
    pre_x1 = red3[rows:]
    dpre0 = dact0 * 2.0 * pos0
    dpreb0 = dpre0.astype(jnp.bfloat16)
    gbe0 = jnp.sum(dpre0, axis=0)

    delta0 = -rate * pen * asum0[:, None] / lens0
    s0 = 1.0 + delta0
    be1 = enc_bias - rate * gbe0
    corr = jnp.dot(gram10, dpreb0.astype(jnp.float32), precision=HI)
    pre1 = pre_x1 - rate * corr + be1
    pos1 = jnp.maximum(pre1, 0.0)
    act1 = pos1 * pos1
    actb1 = act1.astype(jnp.bfloat16)
    asum1 = jnp.sum(act1, axis=0)
    actb0f = actb0.astype(jnp.float32)
    actb1f = actb1.astype(jnp.float32)
    h10 = jnp.dot(actb1f, actb0f.T, precision=HI)
    rec1_part = rec1_dot(actb1, delta0, wd_flat, lay, width) - c1 * jnp.dot(h10, errb0.astype(jnp.float32), precision=HI)
    rec1 = allreduce(rec1_part, "feat", n_feat)
    errb1 = (rec1 - x1f).astype(jnp.bfloat16)

    e0f = errb0.astype(jnp.float32).reshape(rows, lay, width)
    e1f = errb1.astype(jnp.float32).reshape(rows, lay, width)
    g00 = jnp.einsum("rld,sld->lrs", e0f, e0f, precision=HI)
    g10 = jnp.einsum("rld,sld->lrs", e1f, e0f, precision=HI)
    cross = jnp.einsum("rj,lrj->jl", actb0f, d0, precision=HI)
    quad = jnp.einsum("rj,lrs,sj->jl", actb0f, g00, actb0f, precision=HI)
    sq1 = s0 * s0 * sq0 - 2.0 * c1 * s0 * cross + c1 * c1 * quad
    lens1 = jnp.sqrt(jnp.maximum(sq1, 0.0) + eps)

    d1 = per_layer_dot(errb1, wd_flat, lay, width)
    lowr = jnp.einsum("lrs,sj->lrj", g10, actb0f, precision=HI)
    dd1 = s0.T[:, None, :] * d1 - c1 * lowr
    dact1_part = cst * jnp.sum(dd1, axis=0) + pen * jnp.sum(lens1, axis=1)[None, :]

    g0 = cst - pen * c1 * asum1[:, None] / lens1
    hcoef = pen * (asum0[:, None] / lens0 + asum1[:, None] * s0 / lens1)
    lhs0 = g0.T[:, :, None] * actb0f.T[None, :, :]
    hi0, lo0 = split_bf16(lhs0)
    lhs1 = jnp.broadcast_to((cst * actb1f).T.astype(jnp.bfloat16)[None], (lay, feats, rows))
    lhs = jnp.concatenate([lhs1, hi0, lo0], axis=2)
    lhs_int, h_int = dec_prep(lhs, hcoef)
    rhs = jnp.concatenate([errb1, errb0, errb0], axis=0)
    rhs_st = rhs.reshape(3 * rows, lay, width).transpose(1, 0, 2).reshape(lay * 3 * rows, width)
    x = dact1_part
    dec_step = None
    k = 1
    part = 0
    while k < n_layer:
        x, lhs_int, rhs_st, h_int = lax.optimization_barrier((x, lhs_int, rhs_st, h_int))
        got = lax.ppermute(x, "layer", [(i, i ^ k) for i in range(n_layer)])
        if part < 2:
            dec_step = dec_call(lhs_int, rhs_st, h_int, dec_weight, part, 2, dec_step)
            part += 1
        x = x + got
        x, dec_step = lax.optimization_barrier((x, dec_step))
        k *= 2
    while part < 2:
        dec_step = dec_call(lhs_int, rhs_st, h_int, dec_weight, part, 2, dec_step)
        part += 1
    dact1 = x

    dpre1 = dact1 * 2.0 * pos1
    dpreb1 = dpre1.astype(jnp.bfloat16)
    gbe1 = jnp.sum(dpre1, axis=0)

    dp = jnp.concatenate([dpreb0, dpreb1], axis=0)
    enc = lax.dot_general(xg.reshape(nb * rows, lw), dp, (((0,), (0,)), ((), ())), preferred_element_type=jnp.float32)
    enc_step = enc.astype(jnp.bfloat16).reshape(lay, width, feats)
    bias_step = gbe0 + gbe1
    return (enc_step, dec_step, bias_step)


def solution(mesh):
    n_layer = mesh.shape["layer"]
    n_feat = mesh.shape["feat"]
    in_specs = (
        P(None, "feat", "layer", None),
        P("layer", None, "feat"),
        P("feat", "layer", None),
        P("feat"),
    )
    out_specs = (P("layer", None, "feat"), P("feat", "layer", None), P("feat"))

    def body(a, we, wd, be):
        return per_device(a, we, wd, be, n_layer, n_feat)

    return jax.shard_map(body, mesh=mesh, in_specs=in_specs, out_specs=out_specs, check_vma=False)
```

```python
import jax
import jax.numpy as jnp
from jax import lax
from jax.experimental import pallas as pl
from jax.sharding import PartitionSpec as P

rate = 0.01
penalty = 2.0
eps = 1e-06
HI = lax.Precision.HIGHEST


def normalize(x):
    xf = x.astype(jnp.float32)
    scale = jnp.sqrt(jnp.mean(xf * xf, axis=-1, keepdims=True) + eps)
    return (xf / scale).astype(jnp.bfloat16)


def allreduce(x, axis, n):
    k = 1
    while k < n:
        x = x + lax.ppermute(x, axis, [(i, i ^ k) for i in range(n)])
        k *= 2
    return x


def allgather_rows(x, axis, n):
    me = lax.axis_index(axis)
    k = 1
    while k < n:
        got = lax.ppermute(x, axis, [(i, i ^ k) for i in range(n)])
        low = (me // k) % 2 == 0
        x = jnp.where(low, jnp.concatenate([x, got], axis=1), jnp.concatenate([got, x], axis=1))
        k *= 2
    return x


def split_bf16(v):
    hi = v.astype(jnp.bfloat16)
    lo = (v - hi.astype(jnp.float32)).astype(jnp.bfloat16)
    return hi, lo


def block_rows(e, lay, width):
    rows = e.shape[0]
    e3 = e.reshape(rows, lay, width)
    eye = jnp.eye(lay, dtype=e.dtype)
    blk = eye[:, None, :, None] * e3[None, :, :, :]
    return blk.reshape(lay * rows, lay * width)


def per_layer_dot(e, wd2, lay, width):
    outs = []
    for l in range(lay):
        cols = slice(l * width, (l + 1) * width)
        outs.append(lax.dot_general(wd2[:, cols], e[:, cols], (((1,), (1,)), ((), ())), preferred_element_type=jnp.float32))
    return jnp.stack(outs, axis=0).transpose(0, 2, 1)


def rec1_dot(actb1, delta, wd2, lay, width):
    rows = actb1.shape[0]
    parts = []
    for l in range(lay):
        cols = slice(l * width, (l + 1) * width)
        corr = (actb1.astype(jnp.float32) * delta[:, l][None, :]).astype(jnp.bfloat16)
        out = jnp.dot(jnp.concatenate([actb1, corr], axis=0), wd2[:, cols], preferred_element_type=jnp.float32)
        parts.append(out[:rows] + out[rows:])
    return jnp.concatenate(parts, axis=1)


def dec_kernel(lhs_ref, rhs_ref, h_ref, wd_ref, out_ref):
    tj, lay, width = wd_ref.shape
    acc = jnp.dot(lhs_ref[...], rhs_ref[...], preferred_element_type=jnp.float32)
    w = wd_ref[...].reshape(tj * lay, width).astype(jnp.float32)
    acc = acc + h_ref[:, 0:1] * w
    out_ref[...] = acc.astype(out_ref.dtype).reshape(tj, lay, width)


def dec_prep(lhs, hcoef):
    lay, feats, k = lhs.shape
    eye = jnp.eye(lay, dtype=lhs.dtype)
    lhs_int = (eye[None, :, :, None] * lhs.transpose(1, 0, 2)[:, :, None, :]).reshape(feats * lay, lay * k)
    h_int = jnp.broadcast_to(hcoef.reshape(feats * lay, 1), (feats * lay, 128))
    return lhs_int, h_int


def dec_kernel_acc(lhs_ref, rhs_ref, h_ref, wd_ref, prev_ref, out_ref):
    del prev_ref
    dec_kernel(lhs_ref, rhs_ref, h_ref, wd_ref, out_ref)


def dec_call(lhs_int, rhs_st, h_int, wd, part, parts, prev=None):
    feats, lay, width = wd.shape
    k2 = lhs_int.shape[1]
    tj = min(512, feats // parts)
    steps = feats // parts // tj
    off = part * steps
    cost = pl.CostEstimate(
        flops=2 * feats * lay * width * k2 // parts, transcendentals=0, bytes_accessed=4 * feats * lay * width // parts
    )
    in_specs = [
        pl.BlockSpec((tj * lay, k2), lambda j: (j + off, 0)),
        pl.BlockSpec((k2, width), lambda j: (0, 0)),
        pl.BlockSpec((tj * lay, 128), lambda j: (j + off, 0)),
        pl.BlockSpec((tj, lay, width), lambda j: (j + off, 0, 0)),
    ]
    args = [lhs_int, rhs_st, h_int, wd]
    kern, aliases = dec_kernel, {}
    if prev is not None:
        in_specs.append(pl.BlockSpec(memory_space=pl.ANY))
        args.append(prev)
        kern, aliases = dec_kernel_acc, {4: 0}
    return pl.pallas_call(
        kern,
        grid=(steps,),
        in_specs=in_specs,
        out_specs=pl.BlockSpec((tj, lay, width), lambda j: (j + off, 0, 0)),
        out_shape=jax.ShapeDtypeStruct((feats, lay, width), jnp.bfloat16),
        input_output_aliases=aliases,
        cost_estimate=cost,
    )(*args)


def per_device(activations, enc_weight, dec_weight, enc_bias, n_layer, n_feat):
    nb, rloc, lay, width = activations.shape
    feats = enc_weight.shape[2]
    lw = lay * width
    rows = rloc * n_feat
    cst = 2.0 / rows
    pen = penalty / rows
    c1 = rate * cst

    xn = normalize(activations).reshape(nb, rloc, lw)
    xg = allgather_rows(xn, "feat", n_feat)
    x0, x1 = xg[0], xg[1]
    x0f = x0.astype(jnp.float32)
    x1f = x1.astype(jnp.float32)

    we_flat = enc_weight.reshape(lw, feats)
    wd_flat = dec_weight.reshape(feats, lw)

    pre_part = jnp.dot(xg.reshape(nb * rows, lw), we_flat, preferred_element_type=jnp.float32)
    gram = lax.dot_general(x1, x0, (((1,), (1,)), ((), ())), preferred_element_type=jnp.float32)
    gk = -(-(rows * rows) // feats)
    gpad = jnp.pad(gram.reshape(-1), (0, gk * feats - rows * rows)).reshape(gk, feats)
    red1 = allreduce(jnp.concatenate([pre_part[:rows], gpad], axis=0), "layer", n_layer)
    pre_x0 = red1[:rows]
    gram10 = red1[rows:].reshape(-1)[: rows * rows].reshape(rows, rows)
    pre_x1_part = pre_part[rows:]

    sq0 = jnp.stack(
        [jnp.sum(jnp.square(wd_flat[:, l * width : (l + 1) * width].astype(jnp.float32)), axis=1) for l in range(lay)],
        axis=1,
    )
    lens0 = jnp.sqrt(sq0 + eps)

    pre0 = pre_x0 + enc_bias
    pos0 = jnp.maximum(pre0, 0.0)
    act0 = pos0 * pos0
    actb0 = act0.astype(jnp.bfloat16)
    asum0 = jnp.sum(act0, axis=0)
    rec0 = allreduce(jnp.dot(actb0, wd_flat, preferred_element_type=jnp.float32), "feat", n_feat)
    errb0 = (rec0 - x0f).astype(jnp.bfloat16)
    d0 = per_layer_dot(errb0, wd_flat, lay, width)
    dact0_part = cst * jnp.sum(d0, axis=0) + pen * jnp.sum(lens0, axis=1)[None, :]
    red3 = allreduce(jnp.concatenate([dact0_part, pre_x1_part], axis=0), "layer", n_layer)
    dact0 = red3[:rows]
    pre_x1 = red3[rows:]
    dpre0 = dact0 * 2.0 * pos0
    dpreb0 = dpre0.astype(jnp.bfloat16)
    gbe0 = jnp.sum(dpre0, axis=0)

    delta0 = -rate * pen * asum0[:, None] / lens0
    s0 = 1.0 + delta0
    be1 = enc_bias - rate * gbe0
    corr = jnp.dot(gram10, dpreb0.astype(jnp.float32), precision=HI)
    pre1 = pre_x1 - rate * corr + be1
    pos1 = jnp.maximum(pre1, 0.0)
    act1 = pos1 * pos1
    actb1 = act1.astype(jnp.bfloat16)
    asum1 = jnp.sum(act1, axis=0)
    actb0f = actb0.astype(jnp.float32)
    actb1f = actb1.astype(jnp.float32)
    h10 = jnp.dot(actb1f, actb0f.T, precision=HI)
    rec1_part = rec1_dot(actb1, delta0, wd_flat, lay, width) - c1 * jnp.dot(h10, errb0.astype(jnp.float32), precision=HI)

    e0f = errb0.astype(jnp.float32).reshape(rows, lay, width)
    g00 = jnp.einsum("rld,sld->lrs", e0f, e0f, precision=HI)
    cross = jnp.einsum("rj,lrj->jl", actb0f, d0, precision=HI)
    quad = jnp.einsum("rj,lrs,sj->jl", actb0f, g00, actb0f, precision=HI)
    sq1 = s0 * s0 * sq0 - 2.0 * c1 * s0 * cross + c1 * c1 * quad
    lens1 = jnp.sqrt(jnp.maximum(sq1, 0.0) + eps)

    g0 = cst - pen * c1 * asum1[:, None] / lens1
    hcoef = pen * (asum0[:, None] / lens0 + asum1[:, None] * s0 / lens1)
    lhs0 = g0.T[:, :, None] * actb0f.T[None, :, :]
    hi0, lo0 = split_bf16(lhs0)
    lhs1 = jnp.broadcast_to((cst * actb1f).T.astype(jnp.bfloat16)[None], (lay, feats, rows))
    lhs = jnp.concatenate([lhs1, hi0, lo0], axis=2)
    lhs_int, h_int = dec_prep(lhs, hcoef)
    rec1_part, lhs_int, h_int = lax.optimization_barrier((rec1_part, lhs_int, h_int))
    rec1 = allreduce(rec1_part, "feat", n_feat)
    errb1 = (rec1 - x1f).astype(jnp.bfloat16)
    e1f = errb1.astype(jnp.float32).reshape(rows, lay, width)
    g10 = jnp.einsum("rld,sld->lrs", e1f, e0f, precision=HI)
    d1 = per_layer_dot(errb1, wd_flat, lay, width)
    lowr = jnp.einsum("lrs,sj->lrj", g10, actb0f, precision=HI)
    dd1 = s0.T[:, None, :] * d1 - c1 * lowr
    dact1_part = cst * jnp.sum(dd1, axis=0) + pen * jnp.sum(lens1, axis=1)[None, :]

    rhs = jnp.concatenate([errb1, errb0, errb0], axis=0)
    rhs_st = rhs.reshape(3 * rows, lay, width).transpose(1, 0, 2).reshape(lay * 3 * rows, width)
    x = dact1_part
    dec_step = None
    k = 1
    part = 0
    while k < n_layer:
        x, lhs_int, rhs_st, h_int = lax.optimization_barrier((x, lhs_int, rhs_st, h_int))
        got = lax.ppermute(x, "layer", [(i, i ^ k) for i in range(n_layer)])
        if part < 2:
            dec_step = dec_call(lhs_int, rhs_st, h_int, dec_weight, part, 2, dec_step)
            part += 1
        x = x + got
        x, dec_step = lax.optimization_barrier((x, dec_step))
        k *= 2
    while part < 2:
        dec_step = dec_call(lhs_int, rhs_st, h_int, dec_weight, part, 2, dec_step)
        part += 1
    dact1 = x

    dpre1 = dact1 * 2.0 * pos1
    dpreb1 = dpre1.astype(jnp.bfloat16)
    gbe1 = jnp.sum(dpre1, axis=0)

    dp = jnp.concatenate([dpreb0, dpreb1], axis=0)
    enc = lax.dot_general(xg.reshape(nb * rows, lw), dp, (((0,), (0,)), ((), ())), preferred_element_type=jnp.float32)
    enc_step = enc.astype(jnp.bfloat16).reshape(lay, width, feats)
    bias_step = gbe0 + gbe1
    return (enc_step, dec_step, bias_step)


def solution(mesh):
    n_layer = mesh.shape["layer"]
    n_feat = mesh.shape["feat"]
    in_specs = (
        P(None, "feat", "layer", None),
        P("layer", None, "feat"),
        P("feat", "layer", None),
        P("feat"),
    )
    out_specs = (P("layer", None, "feat"), P("feat", "layer", None), P("feat"))

    def body(a, we, wd, be):
        return per_device(a, we, wd, be, n_layer, n_feat)

    return jax.shard_map(body, mesh=mesh, in_specs=in_specs, out_specs=out_specs, check_vma=False)
```

```python
import jax
import jax.numpy as jnp
from jax import lax
from jax.experimental import pallas as pl
from jax.sharding import PartitionSpec as P

rate = 0.01
penalty = 2.0
eps = 1e-06
HI = lax.Precision.HIGHEST


def normalize(x):
    xf = x.astype(jnp.float32)
    scale = jnp.sqrt(jnp.mean(xf * xf, axis=-1, keepdims=True) + eps)
    return (xf / scale).astype(jnp.bfloat16)


def allreduce(x, axis, n):
    k = 1
    while k < n:
        x = x + lax.ppermute(x, axis, [(i, i ^ k) for i in range(n)])
        k *= 2
    return x


def allgather_rows(x, axis, n):
    me = lax.axis_index(axis)
    k = 1
    while k < n:
        got = lax.ppermute(x, axis, [(i, i ^ k) for i in range(n)])
        low = (me // k) % 2 == 0
        x = jnp.concatenate([jnp.where(low, x, got), jnp.where(low, got, x)], axis=1)
        k *= 2
    return x


def split_bf16(v):
    hi = v.astype(jnp.bfloat16)
    lo = (v - hi.astype(jnp.float32)).astype(jnp.bfloat16)
    return hi, lo


def block_rows(e, lay, width):
    rows = e.shape[0]
    e3 = e.reshape(rows, lay, width)
    eye = jnp.eye(lay, dtype=e.dtype)
    blk = eye[:, None, :, None] * e3[None, :, :, :]
    return blk.reshape(lay * rows, lay * width)


def per_layer_dot(e, wd2, lay, width):
    outs = []
    for l in range(lay):
        cols = slice(l * width, (l + 1) * width)
        outs.append(lax.dot_general(wd2[:, cols], e[:, cols], (((1,), (1,)), ((), ())), preferred_element_type=jnp.float32))
    return jnp.stack(outs, axis=0).transpose(0, 2, 1)


def rec1_dot(actb1, delta, wd2, lay, width):
    rows = actb1.shape[0]
    parts = []
    for l in range(lay):
        cols = slice(l * width, (l + 1) * width)
        corr = (actb1.astype(jnp.float32) * delta[:, l][None, :]).astype(jnp.bfloat16)
        out = jnp.dot(jnp.concatenate([actb1, corr], axis=0), wd2[:, cols], preferred_element_type=jnp.float32)
        parts.append(out[:rows] + out[rows:])
    return jnp.concatenate(parts, axis=1)


def dec_kernel(lhs_ref, rhs_ref, h_ref, wd_ref, out_ref):
    tj, lay, width = wd_ref.shape
    acc = jnp.dot(lhs_ref[...], rhs_ref[...], preferred_element_type=jnp.float32)
    w = wd_ref[...].reshape(tj * lay, width).astype(jnp.float32)
    acc = acc + h_ref[:, 0:1] * w
    out_ref[...] = acc.astype(out_ref.dtype).reshape(tj, lay, width)


def dec_prep(lhs, hcoef):
    lay, feats, k = lhs.shape
    eye = jnp.eye(lay, dtype=lhs.dtype)
    lhs_int = (eye[None, :, :, None] * lhs.transpose(1, 0, 2)[:, :, None, :]).reshape(feats * lay, lay * k)
    h_int = jnp.broadcast_to(hcoef.reshape(feats * lay, 1), (feats * lay, 128))
    return lhs_int, h_int


def dec_kernel_acc(lhs_ref, rhs_ref, h_ref, wd_ref, prev_ref, out_ref):
    del prev_ref
    dec_kernel(lhs_ref, rhs_ref, h_ref, wd_ref, out_ref)


def dec_call(lhs_int, rhs_st, h_int, wd, part, parts, prev=None):
    feats, lay, width = wd.shape
    k2 = lhs_int.shape[1]
    tj = min(512, feats // parts)
    steps = feats // parts // tj
    off = part * steps
    cost = pl.CostEstimate(
        flops=2 * feats * lay * width * k2 // parts, transcendentals=0, bytes_accessed=4 * feats * lay * width // parts
    )
    in_specs = [
        pl.BlockSpec((tj * lay, k2), lambda j: (j + off, 0)),
        pl.BlockSpec((k2, width), lambda j: (0, 0)),
        pl.BlockSpec((tj * lay, 128), lambda j: (j + off, 0)),
        pl.BlockSpec((tj, lay, width), lambda j: (j + off, 0, 0)),
    ]
    args = [lhs_int, rhs_st, h_int, wd]
    kern, aliases = dec_kernel, {}
    if prev is not None:
        in_specs.append(pl.BlockSpec(memory_space=pl.ANY))
        args.append(prev)
        kern, aliases = dec_kernel_acc, {4: 0}
    return pl.pallas_call(
        kern,
        grid=(steps,),
        in_specs=in_specs,
        out_specs=pl.BlockSpec((tj, lay, width), lambda j: (j + off, 0, 0)),
        out_shape=jax.ShapeDtypeStruct((feats, lay, width), jnp.bfloat16),
        input_output_aliases=aliases,
        cost_estimate=cost,
    )(*args)


def per_device(activations, enc_weight, dec_weight, enc_bias, n_layer, n_feat):
    nb, rloc, lay, width = activations.shape
    feats = enc_weight.shape[2]
    lw = lay * width
    rows = rloc * n_feat
    cst = 2.0 / rows
    pen = penalty / rows
    c1 = rate * cst

    xn = normalize(activations).reshape(nb, rloc, lw)
    xg = allgather_rows(xn, "feat", n_feat)
    x0, x1 = xg[0], xg[1]
    x0f = x0.astype(jnp.float32)
    x1f = x1.astype(jnp.float32)

    we_flat = enc_weight.reshape(lw, feats)
    wd_flat = dec_weight.reshape(feats, lw)

    pre_part = jnp.dot(xg.reshape(nb * rows, lw), we_flat, preferred_element_type=jnp.float32)
    gram = lax.dot_general(x1, x0, (((1,), (1,)), ((), ())), preferred_element_type=jnp.float32)
    gk = -(-(rows * rows) // feats)
    gpad = jnp.pad(gram.reshape(-1), (0, gk * feats - rows * rows)).reshape(gk, feats)
    red1 = allreduce(jnp.concatenate([pre_part[:rows], gpad], axis=0), "layer", n_layer)
    pre_x0 = red1[:rows]
    gram10 = red1[rows:].reshape(-1)[: rows * rows].reshape(rows, rows)
    pre_x1_part = pre_part[rows:]

    sq0 = jnp.stack(
        [jnp.sum(jnp.square(wd_flat[:, l * width : (l + 1) * width].astype(jnp.float32)), axis=1) for l in range(lay)],
        axis=1,
    )
    lens0 = jnp.sqrt(sq0 + eps)

    pre0 = pre_x0 + enc_bias
    pos0 = jnp.maximum(pre0, 0.0)
    act0 = pos0 * pos0
    actb0 = act0.astype(jnp.bfloat16)
    asum0 = jnp.sum(act0, axis=0)
    rec0 = allreduce(jnp.dot(actb0, wd_flat, preferred_element_type=jnp.float32), "feat", n_feat)
    errb0 = (rec0 - x0f).astype(jnp.bfloat16)
    d0 = per_layer_dot(errb0, wd_flat, lay, width)
    dact0_part = cst * jnp.sum(d0, axis=0) + pen * jnp.sum(lens0, axis=1)[None, :]
    red3 = allreduce(jnp.concatenate([dact0_part, pre_x1_part], axis=0), "layer", n_layer)
    dact0 = red3[:rows]
    pre_x1 = red3[rows:]
    dpre0 = dact0 * 2.0 * pos0
    dpreb0 = dpre0.astype(jnp.bfloat16)
    gbe0 = jnp.sum(dpre0, axis=0)

    delta0 = -rate * pen * asum0[:, None] / lens0
    s0 = 1.0 + delta0
    be1 = enc_bias - rate * gbe0
    corr = jnp.dot(gram10, dpreb0.astype(jnp.float32), precision=HI)
    pre1 = pre_x1 - rate * corr + be1
    pos1 = jnp.maximum(pre1, 0.0)
    act1 = pos1 * pos1
    actb1 = act1.astype(jnp.bfloat16)
    asum1 = jnp.sum(act1, axis=0)
    actb0f = actb0.astype(jnp.float32)
    actb1f = actb1.astype(jnp.float32)
    h10 = jnp.dot(actb1f, actb0f.T, precision=HI)
    rec1_part = rec1_dot(actb1, delta0, wd_flat, lay, width) - c1 * jnp.dot(h10, errb0.astype(jnp.float32), precision=HI)
    rec1 = allreduce(rec1_part, "feat", n_feat)
    errb1 = (rec1 - x1f).astype(jnp.bfloat16)

    e0f = errb0.astype(jnp.float32).reshape(rows, lay, width)
    e1f = errb1.astype(jnp.float32).reshape(rows, lay, width)
    g00 = jnp.einsum("rld,sld->lrs", e0f, e0f, precision=HI)
    g10 = jnp.einsum("rld,sld->lrs", e1f, e0f, precision=HI)
    cross = jnp.einsum("rj,lrj->jl", actb0f, d0, precision=HI)
    quad = jnp.einsum("rj,lrs,sj->jl", actb0f, g00, actb0f, precision=HI)
    sq1 = s0 * s0 * sq0 - 2.0 * c1 * s0 * cross + c1 * c1 * quad
    lens1 = jnp.sqrt(jnp.maximum(sq1, 0.0) + eps)

    d1 = per_layer_dot(errb1, wd_flat, lay, width)
    lowr = jnp.einsum("lrs,sj->lrj", g10, actb0f, precision=HI)
    dd1 = s0.T[:, None, :] * d1 - c1 * lowr
    dact1_part = cst * jnp.sum(dd1, axis=0) + pen * jnp.sum(lens1, axis=1)[None, :]

    g0 = cst - pen * c1 * asum1[:, None] / lens1
    hcoef = pen * (asum0[:, None] / lens0 + asum1[:, None] * s0 / lens1)
    lhs0 = g0.T[:, :, None] * actb0f.T[None, :, :]
    hi0, lo0 = split_bf16(lhs0)
    lhs1 = jnp.broadcast_to((cst * actb1f).T.astype(jnp.bfloat16)[None], (lay, feats, rows))
    lhs = jnp.concatenate([lhs1, hi0, lo0], axis=2)
    lhs_int, h_int = dec_prep(lhs, hcoef)
    rhs = jnp.concatenate([errb1, errb0, errb0], axis=0)
    rhs_st = rhs.reshape(3 * rows, lay, width).transpose(1, 0, 2).reshape(lay * 3 * rows, width)
    x = dact1_part
    dec_step = None
    k = 1
    part = 0
    while k < n_layer:
        x, lhs_int, rhs_st, h_int = lax.optimization_barrier((x, lhs_int, rhs_st, h_int))
        got = lax.ppermute(x, "layer", [(i, i ^ k) for i in range(n_layer)])
        if part < 2:
            dec_step = dec_call(lhs_int, rhs_st, h_int, dec_weight, part, 2, dec_step)
            part += 1
        x = x + got
        x, dec_step = lax.optimization_barrier((x, dec_step))
        k *= 2
    while part < 2:
        dec_step = dec_call(lhs_int, rhs_st, h_int, dec_weight, part, 2, dec_step)
        part += 1
    dact1 = x

    dpre1 = dact1 * 2.0 * pos1
    dpreb1 = dpre1.astype(jnp.bfloat16)
    gbe1 = jnp.sum(dpre1, axis=0)

    dp = jnp.concatenate([dpreb0, dpreb1], axis=0)
    enc = lax.dot_general(xg.reshape(nb * rows, lw), dp, (((0,), (0,)), ((), ())), preferred_element_type=jnp.float32)
    enc_step = enc.astype(jnp.bfloat16).reshape(lay, width, feats)
    bias_step = gbe0 + gbe1
    return (enc_step, dec_step, bias_step)


def solution(mesh):
    n_layer = mesh.shape["layer"]
    n_feat = mesh.shape["feat"]
    in_specs = (
        P(None, "feat", "layer", None),
        P("layer", None, "feat"),
        P("feat", "layer", None),
        P("feat"),
    )
    out_specs = (P("layer", None, "feat"), P("feat", "layer", None), P("feat"))

    def body(a, we, wd, be):
        return per_device(a, we, wd, be, n_layer, n_feat)

    return jax.shard_map(body, mesh=mesh, in_specs=in_specs, out_specs=out_specs, check_vma=False)
```

```python
import jax
import jax.numpy as jnp
from jax import lax
from jax.experimental import pallas as pl
from jax.sharding import PartitionSpec as P

rate = 0.01
penalty = 2.0
eps = 1e-06
HI = lax.Precision.HIGHEST


def normalize(x):
    xf = x.astype(jnp.float32)
    scale = jnp.sqrt(jnp.mean(xf * xf, axis=-1, keepdims=True) + eps)
    return (xf / scale).astype(jnp.bfloat16)


def allreduce(x, axis, n):
    k = 1
    while k < n:
        x = x + lax.ppermute(x, axis, [(i, i ^ k) for i in range(n)])
        k *= 2
    return x


def allgather_rows(x, axis, n):
    me = lax.axis_index(axis)
    k = n // 2
    while k >= 1:
        got = lax.ppermute(x, axis, [(i, i ^ k) for i in range(n)])
        low = (me // k) % 2 == 0
        x = jnp.where(low, jnp.concatenate([x, got], axis=1), jnp.concatenate([got, x], axis=1))
        k //= 2
    return x


def split_bf16(v):
    hi = v.astype(jnp.bfloat16)
    lo = (v - hi.astype(jnp.float32)).astype(jnp.bfloat16)
    return hi, lo


def block_rows(e, lay, width):
    rows = e.shape[0]
    e3 = e.reshape(rows, lay, width)
    eye = jnp.eye(lay, dtype=e.dtype)
    blk = eye[:, None, :, None] * e3[None, :, :, :]
    return blk.reshape(lay * rows, lay * width)


def per_layer_dot(e, wd2, lay, width):
    outs = []
    for l in range(lay):
        cols = slice(l * width, (l + 1) * width)
        outs.append(lax.dot_general(wd2[:, cols], e[:, cols], (((1,), (1,)), ((), ())), preferred_element_type=jnp.float32))
    return jnp.stack(outs, axis=0).transpose(0, 2, 1)


def rec1_dot(actb1, delta, wd2, lay, width):
    rows = actb1.shape[0]
    parts = []
    for l in range(lay):
        cols = slice(l * width, (l + 1) * width)
        corr = (actb1.astype(jnp.float32) * delta[:, l][None, :]).astype(jnp.bfloat16)
        out = jnp.dot(jnp.concatenate([actb1, corr], axis=0), wd2[:, cols], preferred_element_type=jnp.float32)
        parts.append(out[:rows] + out[rows:])
    return jnp.concatenate(parts, axis=1)


def dec_kernel(lhs_ref, rhs_ref, h_ref, wd_ref, out_ref):
    tj, lay, width = wd_ref.shape
    acc = jnp.dot(lhs_ref[...], rhs_ref[...], preferred_element_type=jnp.float32)
    w = wd_ref[...].reshape(tj * lay, width).astype(jnp.float32)
    acc = acc + h_ref[:, 0:1] * w
    out_ref[...] = acc.astype(out_ref.dtype).reshape(tj, lay, width)


def dec_prep(lhs, hcoef):
    lay, feats, k = lhs.shape
    eye = jnp.eye(lay, dtype=lhs.dtype)
    lhs_int = (eye[None, :, :, None] * lhs.transpose(1, 0, 2)[:, :, None, :]).reshape(feats * lay, lay * k)
    h_int = jnp.broadcast_to(hcoef.reshape(feats * lay, 1), (feats * lay, 128))
    return lhs_int, h_int


def dec_kernel_acc(lhs_ref, rhs_ref, h_ref, wd_ref, prev_ref, out_ref):
    del prev_ref
    dec_kernel(lhs_ref, rhs_ref, h_ref, wd_ref, out_ref)


def dec_call(lhs_int, rhs_st, h_int, wd, part, parts, prev=None):
    feats, lay, width = wd.shape
    k2 = lhs_int.shape[1]
    tj = min(512, feats // parts)
    steps = feats // parts // tj
    off = part * steps
    cost = pl.CostEstimate(
        flops=2 * feats * lay * width * k2 // parts, transcendentals=0, bytes_accessed=4 * feats * lay * width // parts
    )
    in_specs = [
        pl.BlockSpec((tj * lay, k2), lambda j: (j + off, 0)),
        pl.BlockSpec((k2, width), lambda j: (0, 0)),
        pl.BlockSpec((tj * lay, 128), lambda j: (j + off, 0)),
        pl.BlockSpec((tj, lay, width), lambda j: (j + off, 0, 0)),
    ]
    args = [lhs_int, rhs_st, h_int, wd]
    kern, aliases = dec_kernel, {}
    if prev is not None:
        in_specs.append(pl.BlockSpec(memory_space=pl.ANY))
        args.append(prev)
        kern, aliases = dec_kernel_acc, {4: 0}
    return pl.pallas_call(
        kern,
        grid=(steps,),
        in_specs=in_specs,
        out_specs=pl.BlockSpec((tj, lay, width), lambda j: (j + off, 0, 0)),
        out_shape=jax.ShapeDtypeStruct((feats, lay, width), jnp.bfloat16),
        input_output_aliases=aliases,
        cost_estimate=cost,
    )(*args)


def per_device(activations, enc_weight, dec_weight, enc_bias, n_layer, n_feat):
    nb, rloc, lay, width = activations.shape
    feats = enc_weight.shape[2]
    lw = lay * width
    rows = rloc * n_feat
    cst = 2.0 / rows
    pen = penalty / rows
    c1 = rate * cst

    xn = normalize(activations).reshape(nb, rloc, lw)
    xg = allgather_rows(xn, "feat", n_feat)
    x0, x1 = xg[0], xg[1]
    x0f = x0.astype(jnp.float32)
    x1f = x1.astype(jnp.float32)

    we_flat = enc_weight.reshape(lw, feats)
    wd_flat = dec_weight.reshape(feats, lw)

    pre_part = jnp.dot(xg.reshape(nb * rows, lw), we_flat, preferred_element_type=jnp.float32)
    gram = lax.dot_general(x1, x0, (((1,), (1,)), ((), ())), preferred_element_type=jnp.float32)
    gk = -(-(rows * rows) // feats)
    gpad = jnp.pad(gram.reshape(-1), (0, gk * feats - rows * rows)).reshape(gk, feats)
    red1 = allreduce(jnp.concatenate([pre_part[:rows], gpad], axis=0), "layer", n_layer)
    pre_x0 = red1[:rows]
    gram10 = red1[rows:].reshape(-1)[: rows * rows].reshape(rows, rows)
    pre_x1_part = pre_part[rows:]

    sq0 = jnp.stack(
        [jnp.sum(jnp.square(wd_flat[:, l * width : (l + 1) * width].astype(jnp.float32)), axis=1) for l in range(lay)],
        axis=1,
    )
    lens0 = jnp.sqrt(sq0 + eps)

    pre0 = pre_x0 + enc_bias
    pos0 = jnp.maximum(pre0, 0.0)
    act0 = pos0 * pos0
    actb0 = act0.astype(jnp.bfloat16)
    asum0 = jnp.sum(act0, axis=0)
    rec0 = allreduce(jnp.dot(actb0, wd_flat, preferred_element_type=jnp.float32), "feat", n_feat)
    errb0 = (rec0 - x0f).astype(jnp.bfloat16)
    d0 = per_layer_dot(errb0, wd_flat, lay, width)
    dact0_part = cst * jnp.sum(d0, axis=0) + pen * jnp.sum(lens0, axis=1)[None, :]
    red3 = allreduce(jnp.concatenate([dact0_part, pre_x1_part], axis=0), "layer", n_layer)
    dact0 = red3[:rows]
    pre_x1 = red3[rows:]
    dpre0 = dact0 * 2.0 * pos0
    dpreb0 = dpre0.astype(jnp.bfloat16)
    gbe0 = jnp.sum(dpre0, axis=0)

    delta0 = -rate * pen * asum0[:, None] / lens0
    s0 = 1.0 + delta0
    be1 = enc_bias - rate * gbe0
    corr = jnp.dot(gram10, dpreb0.astype(jnp.float32), precision=HI)
    pre1 = pre_x1 - rate * corr + be1
    pos1 = jnp.maximum(pre1, 0.0)
    act1 = pos1 * pos1
    actb1 = act1.astype(jnp.bfloat16)
    asum1 = jnp.sum(act1, axis=0)
    actb0f = actb0.astype(jnp.float32)
    actb1f = actb1.astype(jnp.float32)
    h10 = jnp.dot(actb1f, actb0f.T, precision=HI)
    rec1_part = rec1_dot(actb1, delta0, wd_flat, lay, width) - c1 * jnp.dot(h10, errb0.astype(jnp.float32), precision=HI)
    rec1 = allreduce(rec1_part, "feat", n_feat)
    errb1 = (rec1 - x1f).astype(jnp.bfloat16)

    e0f = errb0.astype(jnp.float32).reshape(rows, lay, width)
    e1f = errb1.astype(jnp.float32).reshape(rows, lay, width)
    g00 = jnp.einsum("rld,sld->lrs", e0f, e0f, precision=HI)
    g10 = jnp.einsum("rld,sld->lrs", e1f, e0f, precision=HI)
    cross = jnp.einsum("rj,lrj->jl", actb0f, d0, precision=HI)
    quad = jnp.einsum("rj,lrs,sj->jl", actb0f, g00, actb0f, precision=HI)
    sq1 = s0 * s0 * sq0 - 2.0 * c1 * s0 * cross + c1 * c1 * quad
    lens1 = jnp.sqrt(jnp.maximum(sq1, 0.0) + eps)

    d1 = per_layer_dot(errb1, wd_flat, lay, width)
    lowr = jnp.einsum("lrs,sj->lrj", g10, actb0f, precision=HI)
    dd1 = s0.T[:, None, :] * d1 - c1 * lowr
    dact1_part = cst * jnp.sum(dd1, axis=0) + pen * jnp.sum(lens1, axis=1)[None, :]

    g0 = cst - pen * c1 * asum1[:, None] / lens1
    hcoef = pen * (asum0[:, None] / lens0 + asum1[:, None] * s0 / lens1)
    lhs0 = g0.T[:, :, None] * actb0f.T[None, :, :]
    hi0, lo0 = split_bf16(lhs0)
    lhs1 = jnp.broadcast_to((cst * actb1f).T.astype(jnp.bfloat16)[None], (lay, feats, rows))
    lhs = jnp.concatenate([lhs1, hi0, lo0], axis=2)
    lhs_int, h_int = dec_prep(lhs, hcoef)
    rhs = jnp.concatenate([errb1, errb0, errb0], axis=0)
    rhs_st = rhs.reshape(3 * rows, lay, width).transpose(1, 0, 2).reshape(lay * 3 * rows, width)
    x = dact1_part
    dec_step = None
    k = 1
    part = 0
    while k < n_layer:
        x, lhs_int, rhs_st, h_int = lax.optimization_barrier((x, lhs_int, rhs_st, h_int))
        got = lax.ppermute(x, "layer", [(i, i ^ k) for i in range(n_layer)])
        if part < 2:
            dec_step = dec_call(lhs_int, rhs_st, h_int, dec_weight, part, 2, dec_step)
            part += 1
        x = x + got
        x, dec_step = lax.optimization_barrier((x, dec_step))
        k *= 2
    while part < 2:
        dec_step = dec_call(lhs_int, rhs_st, h_int, dec_weight, part, 2, dec_step)
        part += 1
    dact1 = x

    dpre1 = dact1 * 2.0 * pos1
    dpreb1 = dpre1.astype(jnp.bfloat16)
    gbe1 = jnp.sum(dpre1, axis=0)

    dp = jnp.concatenate([dpreb0, dpreb1], axis=0)
    enc = lax.dot_general(xg.reshape(nb * rows, lw), dp, (((0,), (0,)), ((), ())), preferred_element_type=jnp.float32)
    enc_step = enc.astype(jnp.bfloat16).reshape(lay, width, feats)
    bias_step = gbe0 + gbe1
    return (enc_step, dec_step, bias_step)


def solution(mesh):
    n_layer = mesh.shape["layer"]
    n_feat = mesh.shape["feat"]
    in_specs = (
        P(None, "feat", "layer", None),
        P("layer", None, "feat"),
        P("feat", "layer", None),
        P("feat"),
    )
    out_specs = (P("layer", None, "feat"), P("feat", "layer", None), P("feat"))

    def body(a, we, wd, be):
        return per_device(a, we, wd, be, n_layer, n_feat)

    return jax.shard_map(body, mesh=mesh, in_specs=in_specs, out_specs=out_specs, check_vma=False)
```
